32 devices in a mesh: grp: 4 (over z), emb: 8 (over y, x, core).
Axes of the slice: x: 2, y: 2, z: 4, core: 2. Of those that a mesh axis runs over, the one named last changes fastest.
Arguments:
- bottom_out: bfloat16 [4096, 128], P(('grp', 'emb')), may hold values from -6 to 6
- owner_ids: int32 [106496, 1], P(('grp', 'emb')), may hold values from 0 to 7; in each aligned block of 3328 rows (0 to 3327, 3328 to 6655, ...) at most 624 rows name the same one
- row_ids: int32 [4096, 26], P(('grp', 'emb')), may hold values from 0 to 95
- positions: int32 [4096], P(('grp', 'emb')), may hold values from 0 to 15
- labels: int32 [4096], P(('grp', 'emb')), may hold values 0 or 1
- tables: bfloat16 [26, 768, 128], P(None, 'emb'), may hold values from -6 to 6
- cross_down: bfloat16 [3456, 512], replicated, may hold values from -0.109375 to 0.109375
- cross_up: bfloat16 [512, 3456], replicated, may hold values from -0.25 to 0.25
- cross_bias: float32 [3456], replicated, may hold values from -3 to 3
- out_weight: bfloat16 [3456], replicated, may hold values from -0.109375 to 0.109375
- position_bias: float32 [16], replicated, may hold values from -2 to 2
Outputs:
- table_grad: float32 [26, 768, 128], P(None, 'emb')
- bottom_grad: bfloat16 [4096, 128], P(('grp', 'emb'))
- bias_grad: float32 [3456], replicated
The draws below stay inside these ranges and needn't reach their ends.
Inputs may be any that keep to these rules, and one draw needn't show every extreme that they name: `owner_ids`: in every aligned block of 3328 lookups (the lookups of one device) no owner is named more than 624 times, and in some block one owner is named exactly 624 times.
All inputs are finite; a program needn't handle non-finite values. No bound on the sum of `labels` on one device may be relied on, other than what follows from the above.
Results may differ from the reference program's by a relative error of at most 0.0085.
Values may be sent and summed in bfloat16 or wider, within the bound.
No kernel may reach another device: no remote copies, remote signals or barrier semaphores. Data moves between devices by JAX's collectives and lax.ppermute only.
A program may use at most 64 MiB of HBM per device.

```python
import math
import jax
import jax.numpy as jnp
import numpy as np
from jax import lax

D_EMB = 128
TABLES = 26
RANK = 512
B_DEV = 128
ROWS_DEV = 96
POSITIONS = 16
WIDTH = 3456
ROWS = 768
BATCH = 4096
LOOKUPS = 106496
CAP = 624
N_EMB = 8


def set_ends(result, own_key, smallest, top_value):
    extent = result.shape
    spot = [jax.random.randint(jax.random.fold_in(own_key, axis), (), 0, extent[axis]) for axis in range(len(extent))]
    result = result.at[tuple(spot)].set(smallest)
    longest = extent.index(max(extent))
    spot[longest] = (spot[longest] + 1) % extent[longest]
    return result.at[tuple(spot)].set(top_value)


def steps_of(rng, dims, split, least, high):
    level, own = 1.0, jax.random.fold_in(rng, 6)
    for axis_at, shards_of in split:
        draws = jnp.exp(jax.random.uniform(jax.random.fold_in(own, axis_at), (shards_of,), jnp.float32, least / len(split), high / len(split)))
        level = level * jnp.repeat(draws, dims[axis_at] // shards_of).reshape([-1 if axis == axis_at else 1 for axis in range(len(dims))])
    return level


def rank_table(amount, skew):
    loads = [(1 << 20) // math.isqrt(rank ** skew) + 1 for rank in range(1, amount + 1)]
    deviation = 1 + sum(loads) // (1 << 30)
    return np.cumsum(np.array([max(1, weight // deviation) for weight in loads]))


def skewed_ids(own_key, shape, number_of, slope):
    table = rank_table(number_of, slope)
    ticket = jax.random.randint(jax.random.fold_in(own_key, 1), shape, 0, int(table[number_of - 1]))
    standing = jnp.searchsorted(jnp.asarray(table, jnp.int32), ticket, side="right")
    return jax.random.permutation(jax.random.fold_in(own_key, 2), number_of)[standing].astype(jnp.int32)


def deal_out(rng, own, number, rows, number_of, top, most, slope):
    order = jax.random.permutation(rng, number_of)
    crowded, ordinary = portions_of(number_of, rows * top, most, slope, True), portions_of(number_of, rows * top, most, slope, False)
    places = jnp.arange(number_of)

    def named(sizes, turn):
        used = int((sizes > 0).sum())
        fixed = max(1, used // 4)
        shifted = fixed + (places - fixed + turn * (used - fixed)) % max(1, number_of - fixed)
        return jnp.zeros((number_of,), jnp.int32).at[order[jnp.where(places < fixed, places, shifted)]].set(jnp.asarray(sizes, jnp.int32))

    sizes = jnp.where(number % 4 == 0, named(crowded, number // 4), named(ordinary, number - number // 4 - 1))
    mixed = jax.random.permutation(jax.random.fold_in(own, 3), number_of)
    donor, receiver = mixed[0:number_of // 2 * 2:2], mixed[1:number_of // 2 * 2:2]
    margin = jnp.minimum(sizes[donor] - 1, most - sizes[receiver]) // 2
    margin = jnp.where((donor == order[0]) | (receiver == order[0]) | (sizes[receiver] == 0), 0, jnp.maximum(margin, 0))
    shifted = jax.random.randint(jax.random.fold_in(own, 4), (number_of // 2,), 0, 1 << 20) % (margin + 1)
    sizes = sizes.at[donor].add(-shifted).at[receiver].add(shifted)
    members = jnp.searchsorted(jnp.cumsum(sizes), jnp.arange(rows * top), side="right").astype(jnp.int32)
    grid = members.reshape(top, rows).T
    grid = grid[jax.random.permutation(jax.random.fold_in(own, 1), rows)]
    turn = jax.random.randint(jax.random.fold_in(own, 2), (rows, 1), 0, top)
    return jnp.take_along_axis(grid, (jnp.arange(top)[None, :] + turn) % top, axis=1)


def portions_of(number_of, total, bound, lean, full):
    weights = [(1 << 20) // math.isqrt(rank ** lean) + 1 for rank in range(1, number_of + 1)]
    largest = bound if full else min(bound, max(-(-total // number_of), total * weights[0] // sum(weights)))
    least = 1 if total - largest >= number_of - 1 else 0
    given, rest = [largest] + [least] * (number_of - 1), total - largest - least * (number_of - 1)
    while rest > 0:
        free = [i for i in range(1, number_of) if given[i] < largest] or [i for i in range(1, number_of) if given[i] < bound]
        mass, left = sum([weights[i] for i in free]), rest
        for i in free:
            extra = min(bound - given[i], max(1, left * weights[i] // mass), rest)
            given[i] = given[i] + extra
            rest = rest - extra
    return np.array(given)


def centred(stream_key, shape, deviation, limit, pieces=(), kind=jnp.bfloat16):
    loudness = steps_of(stream_key, shape, pieces, -0.22, 0.18) if pieces else 1.0
    result = jax.random.normal(stream_key, shape, jnp.float32) * deviation * loudness
    return jnp.minimum(jnp.maximum(result, -limit), limit).astype(kind)


def setup_inputs(seed: int = 0) -> dict:
    splits = jax.random.split(jax.random.key(seed), 12)
    bottom_out = centred(splits[0], (BATCH, D_EMB), 1.0, 6.0, ((0, 32),))
    owner_ids_keys = jax.random.split(jax.random.fold_in(splits[1], 1), LOOKUPS // (B_DEV * TABLES))
    owner_ids_turns = jax.random.permutation(jax.random.fold_in(splits[1], 3), LOOKUPS // (B_DEV * TABLES))
    owner_ids = jax.vmap(lambda own, number: deal_out(jax.random.fold_in(splits[1], 2), own, number, B_DEV * TABLES, N_EMB, 1, CAP, 2))(owner_ids_keys, owner_ids_turns).reshape((LOOKUPS, 1))
    row_ids = set_ends(skewed_ids(splits[2], (BATCH, TABLES), ROWS_DEV, 1), jax.random.fold_in(splits[2], 3), 0, ROWS_DEV - 1).astype(jnp.int32)
    positions = set_ends(jax.random.randint(splits[3], (BATCH,), 0, POSITIONS), jax.random.fold_in(splits[3], 1), 0, POSITIONS - 1).astype(jnp.int32)
    labels = set_ends((jax.random.randint(splits[4], (BATCH,), 0, 4) < 1).astype(jnp.int32), jax.random.fold_in(splits[4], 1), 0, 1)
    tables = centred(splits[5], (TABLES, ROWS, D_EMB), 1.0, 6.0, ((1, 8),))
    cross_down = centred(splits[6], (WIDTH, RANK), WIDTH ** -0.5, 0.109375)
    cross_up = centred(splits[7], (RANK, WIDTH), RANK ** -0.5, 0.25)
    cross_bias = centred(splits[8], (WIDTH,), 0.5, 3.0, (), jnp.float32)
    out_weight = centred(splits[9], (WIDTH,), WIDTH ** -0.5, 0.109375)
    position_bias = jnp.clip(jax.random.uniform(splits[10], (POSITIONS,), jnp.float32, -2.0, 2.0), -2.0, 2.0)
    return {"bottom_out": bottom_out, "owner_ids": owner_ids, "row_ids": row_ids, "positions": positions, "labels": labels, "tables": tables, "cross_down": cross_down, "cross_up": cross_up, "cross_bias": cross_bias, "out_weight": out_weight, "position_bias": position_bias}


def reference(bottom_out, owner_ids, row_ids, positions, labels, tables, cross_down, cross_up, cross_bias, out_weight, position_bias):
    block_rows = min(2048, BATCH)
    block_count = BATCH // block_rows
    flat_tables = tables.reshape(TABLES * ROWS, D_EMB)
    weight_row = out_weight.astype(jnp.float32)
    table_base = jnp.arange(TABLES, dtype=jnp.int32)[None, :] * ROWS

    def one_block(carry, inputs):
        table_acc, bias_acc = carry
        bottom, owners, fetched_rows, shown, clicked = inputs
        row_index = (table_base + owners * ROWS_DEV + fetched_rows).astype(jnp.int32)
        pooled = flat_tables[row_index.reshape(-1)].reshape(block_rows, TABLES * D_EMB)
        first = jnp.concatenate([bottom, pooled], axis=1)
        first_wide = first.astype(jnp.float32)
        reduced = jnp.dot(first, cross_down, preferred_element_type=jnp.float32).astype(jnp.bfloat16)
        gate_scale = jnp.dot(reduced, cross_up, preferred_element_type=jnp.float32) + cross_bias
        crossed = first_wide * gate_scale + first_wide
        logit = jnp.sum(crossed * weight_row[None, :], axis=1) + position_bias[shown]
        err = jax.nn.sigmoid(logit) - clicked.astype(jnp.float32)
        cotangent = err[:, None] * weight_row[None, :]
        scaled = cotangent * first_wide
        down_grad = jnp.dot(scaled.astype(jnp.bfloat16), cross_up.T, preferred_element_type=jnp.float32).astype(jnp.bfloat16)
        input_grad = (cotangent * (gate_scale + 1.0) + jnp.dot(down_grad, cross_down.T, preferred_element_type=jnp.float32)).astype(jnp.bfloat16)
        row_grads = input_grad[:, D_EMB:].reshape(block_rows * TABLES, D_EMB).astype(jnp.float32)
        table_acc = table_acc.at[row_index.reshape(-1)].add(row_grads)
        bias_acc = bias_acc + jnp.sum(scaled, axis=0)
        return (table_acc, bias_acc), input_grad[:, :D_EMB]

    inputs = (bottom_out.reshape(block_count, block_rows, D_EMB),
              owner_ids.reshape(block_count, block_rows, TABLES),
              row_ids.reshape(block_count, block_rows, TABLES),
              positions.reshape(block_count, block_rows),
              labels.reshape(block_count, block_rows))
    start = (jnp.zeros((TABLES * ROWS, D_EMB), jnp.float32), jnp.zeros((WIDTH,), jnp.float32))
    (table_acc, bias_acc), bottom_parts = lax.scan(one_block, start, inputs)
    return table_acc.reshape(TABLES, ROWS, D_EMB), bottom_parts.reshape(BATCH, D_EMB), bias_acc
```

```python
import jax
import jax.numpy as jnp
from jax import lax
from jax.sharding import PartitionSpec as P


def local(
    bottom_out,
    owner_ids,
    row_ids,
    positions,
    labels,
    tables,
    cross_down,
    cross_up,
    cross_bias,
    out_weight,
    position_bias,
):
    sample_count, table_count = row_ids.shape
    rows_local = tables.shape[1]
    row_width = tables.shape[2]
    owner_count = lax.axis_size("emb")
    capacity = 3 * sample_count * table_count // (2 * owner_count)
    lookup_count = sample_count * table_count
    owners = owner_ids.reshape(sample_count, table_count)
    flat_owner = owners.reshape(-1)
    local_grid = jnp.arange(table_count, dtype=jnp.int32)[None, :] * rows_local + row_ids
    local_index = local_grid.reshape(-1)
    owner_marks = (flat_owner[:, None] == jnp.arange(owner_count, dtype=jnp.int32)[None, :]).astype(
        jnp.int32
    )
    ranking = jnp.cumsum(owner_marks, axis=0) - 1
    slot_index = jnp.sum(ranking * owner_marks, axis=1)
    buffer_place = flat_owner * capacity + slot_index
    flat_table = tables.reshape(table_count * rows_local, row_width)
    request = jnp.zeros((owner_count * capacity,), jnp.int32).at[buffer_place].set(local_index)
    request = request.reshape(owner_count, capacity)
    received = lax.all_to_all(request, "emb", split_axis=0, concat_axis=0, tiled=True)
    fetched = flat_table[received]
    arrived = lax.all_to_all(fetched, "emb", split_axis=0, concat_axis=0, tiled=True)
    pooled = arrived.reshape(owner_count * capacity, row_width)[buffer_place].reshape(
        sample_count, table_count * row_width
    )
    first = jnp.concatenate([bottom_out, pooled], axis=1)
    first_wide = first.astype(jnp.float32)
    weight_row = out_weight.astype(jnp.float32)
    reduced = jnp.dot(first, cross_down, preferred_element_type=jnp.float32).astype(jnp.bfloat16)
    gate_scale = jnp.dot(reduced, cross_up, preferred_element_type=jnp.float32) + cross_bias
    crossed = first_wide * gate_scale + first_wide
    position_marks = (
        positions[:, None] == jnp.arange(position_bias.shape[0], dtype=jnp.int32)[None, :]
    ).astype(jnp.float32)
    logit = jnp.sum(crossed * weight_row[None, :], axis=1) + jnp.sum(
        position_marks * position_bias[None, :], axis=1
    )
    err = jax.nn.sigmoid(logit) - labels.astype(jnp.float32)
    cotangent = err[:, None] * weight_row[None, :]
    scaled = cotangent * first_wide
    bias_local = jnp.sum(scaled, axis=0)
    down_grad = lax.dot_general(
        scaled.astype(jnp.bfloat16),
        cross_up,
        (((1,), (1,)), ((), ())),
        preferred_element_type=jnp.float32,
    ).astype(jnp.bfloat16)
    back_term = lax.dot_general(
        down_grad, cross_down, (((1,), (1,)), ((), ())), preferred_element_type=jnp.float32
    )
    input_grad = (cotangent * (gate_scale + 1.0) + back_term).astype(jnp.bfloat16)
    bottom_grad = input_grad[:, :row_width]
    row_grads = input_grad[:, row_width:].reshape(lookup_count, row_width)
    outgoing = (
        jnp.zeros((owner_count * capacity, row_width), jnp.bfloat16).at[buffer_place].set(row_grads)
    )
    incoming = lax.all_to_all(
        outgoing.reshape(owner_count, capacity, row_width),
        "emb",
        split_axis=0,
        concat_axis=0,
        tiled=True,
    )
    local_grad = (
        jnp.zeros((table_count * rows_local, row_width), jnp.float32)
        .at[received.reshape(-1)]
        .add(incoming.reshape(owner_count * capacity, row_width).astype(jnp.float32))
    )
    bias_emb = lax.psum(bias_local, "emb")
    packed = jnp.concatenate([local_grad.reshape(-1), bias_emb])
    packed = lax.psum(packed, "grp")
    summed_grad = packed[: local_grad.size].reshape(local_grad.shape)
    bias_grad = packed[local_grad.size :]
    table_grad = summed_grad.reshape(table_count, rows_local, row_width)
    return (table_grad, bottom_grad, bias_grad)


def solution(mesh):
    placed = (
        P(("grp", "emb"), None),
        P(("grp", "emb"), None),
        P(("grp", "emb"), None),
        P(("grp", "emb")),
        P(("grp", "emb")),
        P(None, "emb", None),
        P(),
        P(),
        P(),
        P(),
        P(),
    )
    return jax.shard_map(
        local,
        mesh=mesh,
        in_specs=placed,
        out_specs=(P(None, "emb", None), P(("grp", "emb"), None), P()),
        check_vma=False,
    )
```

```python
import functools

import jax
import jax.numpy as jnp
from jax import lax
from jax.experimental import pallas as pl
from jax.experimental.pallas import tpu as pltpu
from jax.sharding import PartitionSpec as P

CHUNK = 512


def _row_block(rows):
    for size in range(512, 7, -8):
        if rows % size == 0:
            return size
    return rows


def _select_kernel(chunks, left_ref, right_ref, data_ref, out_ref):
    left = left_ref[...]

    def step(j, acc):
        start = pl.multiple_of(j * CHUNK, CHUNK)
        right = right_ref[:, pl.ds(start, CHUNK)]
        picks = jnp.where(left == right, 1.0, 0.0).astype(data_ref.dtype)
        block = data_ref[pl.ds(start, CHUNK), :]
        return acc + jnp.dot(picks, block, preferred_element_type=jnp.float32)

    acc = jnp.zeros(out_ref.shape, jnp.float32)
    acc = lax.fori_loop(0, chunks, step, acc)
    out_ref[...] = acc.astype(out_ref.dtype)


def select_rows(left, right, data, out_dtype):
    rows = left.shape[0]
    count, width = data.shape
    padded = -(-count // CHUNK) * CHUNK
    right = jnp.pad(right, (0, padded - count), constant_values=-1).reshape(1, padded)
    data = jnp.pad(data, ((0, padded - count), (0, 0)))
    block = _row_block(rows)
    return pl.pallas_call(
        functools.partial(_select_kernel, padded // CHUNK),
        out_shape=jax.ShapeDtypeStruct((rows, width), out_dtype),
        grid=(rows // block,),
        in_specs=[
            pl.BlockSpec((block, 1), lambda i: (i, 0)),
            pl.BlockSpec((1, padded), lambda i: (0, 0)),
            pl.BlockSpec((padded, width), lambda i: (0, 0)),
        ],
        out_specs=pl.BlockSpec((block, width), lambda i: (i, 0)),
        cost_estimate=pl.CostEstimate(
            flops=2 * rows * padded * width,
            transcendentals=0,
            bytes_accessed=padded * width * data.dtype.itemsize
            + rows * width * jnp.dtype(out_dtype).itemsize,
        ),
    )(left.reshape(rows, 1), right, data)


def local(
    bottom_out,
    owner_ids,
    row_ids,
    positions,
    labels,
    tables,
    cross_down,
    cross_up,
    cross_bias,
    out_weight,
    position_bias,
):
    sample_count, table_count = row_ids.shape
    rows_local = tables.shape[1]
    row_width = tables.shape[2]
    owner_count = lax.axis_size("emb")
    capacity = 3 * sample_count * table_count // (2 * owner_count)
    lookup_count = sample_count * table_count
    owners = owner_ids.reshape(sample_count, table_count)
    flat_owner = owners.reshape(-1)
    local_grid = jnp.arange(table_count, dtype=jnp.int32)[None, :] * rows_local + row_ids
    local_index = local_grid.reshape(-1)
    owner_marks = (flat_owner[:, None] == jnp.arange(owner_count, dtype=jnp.int32)[None, :]).astype(
        jnp.int32
    )
    ranking = jnp.cumsum(owner_marks, axis=0) - 1
    slot_index = jnp.sum(ranking * owner_marks, axis=1)
    buffer_place = flat_owner * capacity + slot_index
    flat_table = tables.reshape(table_count * rows_local, row_width)
    request = jnp.zeros((owner_count * capacity,), jnp.int32).at[buffer_place].set(local_index)
    request = request.reshape(owner_count, capacity)
    received = lax.all_to_all(request, "emb", split_axis=0, concat_axis=0, tiled=True)
    slot_count = owner_count * capacity
    received_flat = received.reshape(-1)
    fetched = select_rows(
        received_flat, jnp.arange(flat_table.shape[0], dtype=jnp.int32), flat_table, flat_table.dtype
    )
    arrived = lax.all_to_all(fetched, "emb", split_axis=0, concat_axis=0, tiled=True)
    pooled = select_rows(
        buffer_place,
        jnp.arange(slot_count, dtype=jnp.int32),
        arrived.reshape(slot_count, row_width),
        arrived.dtype,
    ).reshape(sample_count, table_count * row_width)
    first = jnp.concatenate([bottom_out, pooled], axis=1)
    first_wide = first.astype(jnp.float32)
    weight_row = out_weight.astype(jnp.float32)
    reduced = jnp.dot(first, cross_down, preferred_element_type=jnp.float32).astype(jnp.bfloat16)
    gate_scale = jnp.dot(reduced, cross_up, preferred_element_type=jnp.float32) + cross_bias
    crossed = first_wide * gate_scale + first_wide
    position_marks = (
        positions[:, None] == jnp.arange(position_bias.shape[0], dtype=jnp.int32)[None, :]
    ).astype(jnp.float32)
    logit = jnp.sum(crossed * weight_row[None, :], axis=1) + jnp.sum(
        position_marks * position_bias[None, :], axis=1
    )
    err = jax.nn.sigmoid(logit) - labels.astype(jnp.float32)
    cotangent = err[:, None] * weight_row[None, :]
    scaled = cotangent * first_wide
    down_grad = lax.dot_general(
        scaled.astype(jnp.bfloat16),
        cross_up,
        (((1,), (1,)), ((), ())),
        preferred_element_type=jnp.float32,
    ).astype(jnp.bfloat16)
    back_term = lax.dot_general(
        down_grad, cross_down, (((1,), (1,)), ((), ())), preferred_element_type=jnp.float32
    )
    input_grad = (cotangent * (gate_scale + 1.0) + back_term).astype(jnp.bfloat16)
    bottom_grad = input_grad[:, :row_width]
    row_grads = input_grad[:, row_width:].reshape(lookup_count, row_width)
    outgoing = select_rows(
        jnp.arange(slot_count, dtype=jnp.int32), buffer_place, row_grads, jnp.bfloat16
    )
    incoming = lax.all_to_all(
        outgoing.reshape(owner_count, capacity, row_width),
        "emb",
        split_axis=0,
        concat_axis=0,
        tiled=True,
    )
    local_grad = select_rows(
        jnp.arange(table_count * rows_local, dtype=jnp.int32),
        received_flat,
        incoming.reshape(slot_count, row_width),
        jnp.float32,
    )
    summed_grad = lax.psum(local_grad.astype(jnp.bfloat16), "grp").astype(jnp.float32)
    table_grad = summed_grad.reshape(table_count, rows_local, row_width)
    bias_local = jnp.sum(scaled, axis=0)
    bias_grad = lax.psum(bias_local, ("grp", "emb"))
    return (table_grad, bottom_grad, bias_grad)


def solution(mesh):
    placed = (
        P(("grp", "emb"), None),
        P(("grp", "emb"), None),
        P(("grp", "emb"), None),
        P(("grp", "emb")),
        P(("grp", "emb")),
        P(None, "emb", None),
        P(),
        P(),
        P(),
        P(),
        P(),
    )
    return jax.shard_map(
        local,
        mesh=mesh,
        in_specs=placed,
        out_specs=(P(None, "emb", None), P(("grp", "emb"), None), P()),
        check_vma=False,
    )
```

```python
import functools

import jax
import jax.numpy as jnp
from jax import lax
from jax.experimental import pallas as pl
from jax.experimental.pallas import tpu as pltpu
from jax.sharding import PartitionSpec as P

CHUNK = 512


def _row_block(rows):
    if rows <= 4096:
        return rows
    for size in range(4096, 7, -8):
        if rows % size == 0:
            return size
    return rows


def _select_kernel(chunks, left_ref, right_ref, data_ref, out_ref):
    left = left_ref[...]

    def step(j, acc):
        start = pl.multiple_of(j * CHUNK, CHUNK)
        right = right_ref[:, pl.ds(start, CHUNK)]
        picks = jnp.where(left == right, 1.0, 0.0).astype(data_ref.dtype)
        block = data_ref[pl.ds(start, CHUNK), :]
        return acc + jnp.dot(picks, block, preferred_element_type=jnp.float32)

    acc = jnp.zeros(out_ref.shape, jnp.float32)
    acc = lax.fori_loop(0, chunks, step, acc)
    out_ref[...] = acc.astype(out_ref.dtype)


def _running_count(marks):
    count, width = marks.shape
    block = 128 if count % 128 == 0 else count
    grouped = marks.reshape(count // block, block, width).astype(jnp.bfloat16)
    lower = (
        jnp.arange(block, dtype=jnp.int32)[:, None] >= jnp.arange(block, dtype=jnp.int32)[None, :]
    ).astype(jnp.bfloat16)
    within = jnp.einsum("rc,bcj->brj", lower, grouped, preferred_element_type=jnp.float32)
    totals = within[:, -1, :]
    before = jnp.cumsum(totals, axis=0) - totals
    return (within + before[:, None, :]).reshape(count, width).astype(jnp.int32)


def select_rows(left, right, data, out_dtype):
    rows = left.shape[0]
    count, width = data.shape
    padded = -(-count // CHUNK) * CHUNK
    right = jnp.pad(right, (0, padded - count), constant_values=-1).reshape(1, padded)
    data = jnp.pad(data, ((0, padded - count), (0, 0)))
    block = _row_block(rows)
    return pl.pallas_call(
        functools.partial(_select_kernel, padded // CHUNK),
        out_shape=jax.ShapeDtypeStruct((rows, width), out_dtype),
        grid=(rows // block,),
        in_specs=[
            pl.BlockSpec((block, 1), lambda i: (i, 0)),
            pl.BlockSpec((1, padded), lambda i: (0, 0)),
            pl.BlockSpec((padded, width), lambda i: (0, 0)),
        ],
        out_specs=pl.BlockSpec((block, width), lambda i: (i, 0)),
        cost_estimate=pl.CostEstimate(
            flops=2 * rows * padded * width,
            transcendentals=0,
            bytes_accessed=padded * width * data.dtype.itemsize
            + rows * width * jnp.dtype(out_dtype).itemsize,
        ),
    )(left.reshape(rows, 1), right, data)


def local(
    bottom_out,
    owner_ids,
    row_ids,
    positions,
    labels,
    tables,
    cross_down,
    cross_up,
    cross_bias,
    out_weight,
    position_bias,
):
    sample_count, table_count = row_ids.shape
    rows_local = tables.shape[1]
    row_width = tables.shape[2]
    owner_count = lax.axis_size("emb")
    capacity = 3 * sample_count * table_count // (2 * owner_count)
    lookup_count = sample_count * table_count
    owners = owner_ids.reshape(sample_count, table_count)
    flat_owner = owners.reshape(-1)
    local_grid = jnp.arange(table_count, dtype=jnp.int32)[None, :] * rows_local + row_ids
    local_index = local_grid.reshape(-1)
    owner_marks = (flat_owner[:, None] == jnp.arange(owner_count, dtype=jnp.int32)[None, :]).astype(
        jnp.int32
    )
    ranking = _running_count(owner_marks) - 1
    slot_index = jnp.sum(ranking * owner_marks, axis=1)
    buffer_place = flat_owner * capacity + slot_index
    flat_table = tables.reshape(table_count * rows_local, row_width)
    request = jnp.zeros((owner_count * capacity,), jnp.int32).at[buffer_place].set(local_index)
    request = request.reshape(owner_count, capacity)
    received = lax.all_to_all(request, "emb", split_axis=0, concat_axis=0, tiled=True)
    slot_count = owner_count * capacity
    received_flat = received.reshape(-1)
    fetched = flat_table[received]
    arrived = lax.all_to_all(fetched, "emb", split_axis=0, concat_axis=0, tiled=True)
    pooled = arrived.reshape(slot_count, row_width)[buffer_place].reshape(
        sample_count, table_count * row_width
    )
    first = jnp.concatenate([bottom_out, pooled], axis=1)
    first_wide = first.astype(jnp.float32)
    weight_row = out_weight.astype(jnp.float32)
    reduced = jnp.dot(first, cross_down, preferred_element_type=jnp.float32).astype(jnp.bfloat16)
    gate_scale = jnp.dot(reduced, cross_up, preferred_element_type=jnp.float32) + cross_bias
    crossed = first_wide * gate_scale + first_wide
    position_marks = (
        positions[:, None] == jnp.arange(position_bias.shape[0], dtype=jnp.int32)[None, :]
    ).astype(jnp.float32)
    logit = jnp.sum(crossed * weight_row[None, :], axis=1) + jnp.sum(
        position_marks * position_bias[None, :], axis=1
    )
    err = jax.nn.sigmoid(logit) - labels.astype(jnp.float32)
    cotangent = err[:, None] * weight_row[None, :]
    scaled = cotangent * first_wide
    down_grad = lax.dot_general(
        scaled.astype(jnp.bfloat16),
        cross_up,
        (((1,), (1,)), ((), ())),
        preferred_element_type=jnp.float32,
    ).astype(jnp.bfloat16)
    back_term = lax.dot_general(
        down_grad, cross_down, (((1,), (1,)), ((), ())), preferred_element_type=jnp.float32
    )
    input_grad = (cotangent * (gate_scale + 1.0) + back_term).astype(jnp.bfloat16)
    bottom_grad = input_grad[:, :row_width]
    row_grads = input_grad[:, row_width:].reshape(lookup_count, row_width)
    outgoing = jnp.zeros((slot_count, row_width), jnp.bfloat16).at[buffer_place].set(row_grads)
    incoming = lax.all_to_all(
        outgoing.reshape(owner_count, capacity, row_width),
        "emb",
        split_axis=0,
        concat_axis=0,
        tiled=True,
    )
    local_grad = select_rows(
        jnp.arange(table_count * rows_local, dtype=jnp.int32),
        received_flat,
        incoming.reshape(slot_count, row_width),
        jnp.float32,
    )
    summed_grad = lax.psum(local_grad.astype(jnp.bfloat16), "grp").astype(jnp.float32)
    table_grad = summed_grad.reshape(table_count, rows_local, row_width)
    bias_local = jnp.sum(scaled, axis=0)
    bias_grad = lax.psum(bias_local, ("grp", "emb"))
    return (table_grad, bottom_grad, bias_grad)


def solution(mesh):
    placed = (
        P(("grp", "emb"), None),
        P(("grp", "emb"), None),
        P(("grp", "emb"), None),
        P(("grp", "emb")),
        P(("grp", "emb")),
        P(None, "emb", None),
        P(),
        P(),
        P(),
        P(),
        P(),
    )
    return jax.shard_map(
        local,
        mesh=mesh,
        in_specs=placed,
        out_specs=(P(None, "emb", None), P(("grp", "emb"), None), P()),
        check_vma=False,
    )
```

```python
import functools

import jax
import jax.numpy as jnp
from jax import lax
from jax.experimental import pallas as pl
from jax.experimental.pallas import tpu as pltpu
from jax.sharding import PartitionSpec as P

CHUNK = 512


def _row_block(rows):
    if rows <= 4096:
        return rows
    for size in range(4096, 7, -8):
        if rows % size == 0:
            return size
    return rows


def _select_kernel(chunks, left_ref, right_ref, data_ref, out_ref):
    left = left_ref[...]

    def step(j, acc):
        start = pl.multiple_of(j * CHUNK, CHUNK)
        right = right_ref[:, pl.ds(start, CHUNK)]
        picks = jnp.where(left == right, 1.0, 0.0).astype(data_ref.dtype)
        block = data_ref[pl.ds(start, CHUNK), :]
        return acc + jnp.dot(picks, block, preferred_element_type=jnp.float32)

    acc = jnp.zeros(out_ref.shape, jnp.float32)
    acc = lax.fori_loop(0, chunks, step, acc)
    out_ref[...] = acc.astype(out_ref.dtype)


def _slot_kernel(capacity, table_count, rows_local, owner_ref, row_ref, place_ref, request_ref, count_ref):
    owner_count = count_ref.shape[0]
    for owner in range(owner_count):
        count_ref[owner] = 0

    def clear(slot, carry):
        request_ref[slot] = 0
        return carry

    lax.fori_loop(0, request_ref.shape[0], clear, 0)

    def assign(lookup, carry):
        owner = owner_ref[lookup]
        taken = count_ref[owner]
        slot = owner * capacity + taken
        count_ref[owner] = taken + 1
        place_ref[lookup] = slot
        request_ref[slot] = (lookup % table_count) * rows_local + row_ref[lookup]
        return carry

    lax.fori_loop(0, owner_ref.shape[0], assign, 0)


def assign_slots(owners, rows, owner_count, capacity, table_count, rows_local):
    lookups = owners.shape[0]
    smem = pltpu.SMEM
    return pl.pallas_call(
        functools.partial(_slot_kernel, capacity, table_count, rows_local),
        out_shape=(
            jax.ShapeDtypeStruct((lookups,), jnp.int32),
            jax.ShapeDtypeStruct((owner_count * capacity,), jnp.int32),
        ),
        in_specs=[pl.BlockSpec(memory_space=smem), pl.BlockSpec(memory_space=smem)],
        out_specs=(pl.BlockSpec(memory_space=smem), pl.BlockSpec(memory_space=smem)),
        scratch_shapes=[pltpu.SMEM((owner_count,), jnp.int32)],
    )(owners, rows)


def _running_count(marks):
    count, width = marks.shape
    block = 128 if count % 128 == 0 else count
    grouped = marks.reshape(count // block, block, width).astype(jnp.bfloat16)
    lower = (
        jnp.arange(block, dtype=jnp.int32)[:, None] >= jnp.arange(block, dtype=jnp.int32)[None, :]
    ).astype(jnp.bfloat16)
    within = jnp.einsum("rc,bcj->brj", lower, grouped, preferred_element_type=jnp.float32)
    totals = within[:, -1, :]
    before = jnp.cumsum(totals, axis=0) - totals
    return (within + before[:, None, :]).reshape(count, width).astype(jnp.int32)


def select_rows(left, right, data, out_dtype):
    rows = left.shape[0]
    count, width = data.shape
    padded = -(-count // CHUNK) * CHUNK
    right = jnp.pad(right, (0, padded - count), constant_values=-1).reshape(1, padded)
    data = jnp.pad(data, ((0, padded - count), (0, 0)))
    block = _row_block(rows)
    return pl.pallas_call(
        functools.partial(_select_kernel, padded // CHUNK),
        out_shape=jax.ShapeDtypeStruct((rows, width), out_dtype),
        grid=(rows // block,),
        in_specs=[
            pl.BlockSpec((block, 1), lambda i: (i, 0)),
            pl.BlockSpec((1, padded), lambda i: (0, 0)),
            pl.BlockSpec((padded, width), lambda i: (0, 0)),
        ],
        out_specs=pl.BlockSpec((block, width), lambda i: (i, 0)),
        cost_estimate=pl.CostEstimate(
            flops=2 * rows * padded * width,
            transcendentals=0,
            bytes_accessed=padded * width * data.dtype.itemsize
            + rows * width * jnp.dtype(out_dtype).itemsize,
        ),
    )(left.reshape(rows, 1), right, data)


def local(
    bottom_out,
    owner_ids,
    row_ids,
    positions,
    labels,
    tables,
    cross_down,
    cross_up,
    cross_bias,
    out_weight,
    position_bias,
):
    sample_count, table_count = row_ids.shape
    rows_local = tables.shape[1]
    row_width = tables.shape[2]
    owner_count = lax.axis_size("emb")
    capacity = 3 * sample_count * table_count // (2 * owner_count)
    lookup_count = sample_count * table_count
    buffer_place, request = assign_slots(
        owner_ids.reshape(-1),
        row_ids.reshape(-1),
        owner_count,
        capacity,
        table_count,
        rows_local,
    )
    flat_table = tables.reshape(table_count * rows_local, row_width)
    request = request.reshape(owner_count, capacity)
    received = lax.all_to_all(request, "emb", split_axis=0, concat_axis=0, tiled=True)
    slot_count = owner_count * capacity
    received_flat = received.reshape(-1)
    fetched = flat_table[received]
    arrived = lax.all_to_all(fetched, "emb", split_axis=0, concat_axis=0, tiled=True)
    pooled = arrived.reshape(slot_count, row_width)[buffer_place].reshape(
        sample_count, table_count * row_width
    )
    first = jnp.concatenate([bottom_out, pooled], axis=1)
    first_wide = first.astype(jnp.float32)
    weight_row = out_weight.astype(jnp.float32)
    reduced = jnp.dot(first, cross_down, preferred_element_type=jnp.float32).astype(jnp.bfloat16)
    gate_scale = jnp.dot(reduced, cross_up, preferred_element_type=jnp.float32) + cross_bias
    crossed = first_wide * gate_scale + first_wide
    position_marks = (
        positions[:, None] == jnp.arange(position_bias.shape[0], dtype=jnp.int32)[None, :]
    ).astype(jnp.float32)
    logit = jnp.sum(crossed * weight_row[None, :], axis=1) + jnp.sum(
        position_marks * position_bias[None, :], axis=1
    )
    err = jax.nn.sigmoid(logit) - labels.astype(jnp.float32)
    cotangent = err[:, None] * weight_row[None, :]
    scaled = cotangent * first_wide
    down_grad = lax.dot_general(
        scaled.astype(jnp.bfloat16),
        cross_up,
        (((1,), (1,)), ((), ())),
        preferred_element_type=jnp.float32,
    ).astype(jnp.bfloat16)
    back_term = lax.dot_general(
        down_grad, cross_down, (((1,), (1,)), ((), ())), preferred_element_type=jnp.float32
    )
    input_grad = (cotangent * (gate_scale + 1.0) + back_term).astype(jnp.bfloat16)
    bottom_grad = input_grad[:, :row_width]
    row_grads = input_grad[:, row_width:].reshape(lookup_count, row_width)
    outgoing = jnp.zeros((slot_count, row_width), jnp.bfloat16).at[buffer_place].set(row_grads)
    incoming = lax.all_to_all(
        outgoing.reshape(owner_count, capacity, row_width),
        "emb",
        split_axis=0,
        concat_axis=0,
        tiled=True,
    )
    local_grad = select_rows(
        jnp.arange(table_count * rows_local, dtype=jnp.int32),
        received_flat,
        incoming.reshape(slot_count, row_width),
        jnp.float32,
    )
    summed_grad = lax.psum(local_grad.astype(jnp.bfloat16), "grp").astype(jnp.float32)
    table_grad = summed_grad.reshape(table_count, rows_local, row_width)
    bias_local = jnp.sum(scaled, axis=0)
    bias_grad = lax.psum(bias_local, ("grp", "emb"))
    return (table_grad, bottom_grad, bias_grad)


def solution(mesh):
    placed = (
        P(("grp", "emb"), None),
        P(("grp", "emb"), None),
        P(("grp", "emb"), None),
        P(("grp", "emb")),
        P(("grp", "emb")),
        P(None, "emb", None),
        P(),
        P(),
        P(),
        P(),
        P(),
    )
    return jax.shard_map(
        local,
        mesh=mesh,
        in_specs=placed,
        out_specs=(P(None, "emb", None), P(("grp", "emb"), None), P()),
        check_vma=False,
    )
```

```python
import functools

import jax
import jax.numpy as jnp
from jax import lax
from jax.experimental import pallas as pl
from jax.experimental.pallas import tpu as pltpu
from jax.sharding import PartitionSpec as P

CHUNK = 512


def _row_block(rows):
    if rows <= 4096:
        return rows
    for size in range(4096, 7, -8):
        if rows % size == 0:
            return size
    return rows


def _select_kernel(chunks, left_ref, right_ref, data_ref, out_ref):
    left = left_ref[...]

    def step(j, acc):
        start = pl.multiple_of(j * CHUNK, CHUNK)
        right = right_ref[:, pl.ds(start, CHUNK)]
        picks = jnp.where(left == right, 1.0, 0.0).astype(data_ref.dtype)
        block = data_ref[pl.ds(start, CHUNK), :]
        return acc + jnp.dot(picks, block, preferred_element_type=jnp.float32)

    acc = jnp.zeros(out_ref.shape, jnp.float32)
    acc = lax.fori_loop(0, chunks, step, acc)
    out_ref[...] = acc.astype(out_ref.dtype)


def _running_count(marks):
    count, width = marks.shape
    block = 128 if count % 128 == 0 else count
    grouped = marks.reshape(count // block, block, width).astype(jnp.bfloat16)
    lower = (
        jnp.arange(block, dtype=jnp.int32)[:, None] >= jnp.arange(block, dtype=jnp.int32)[None, :]
    ).astype(jnp.bfloat16)
    within = jnp.einsum("rc,bcj->brj", lower, grouped, preferred_element_type=jnp.float32)
    totals = within[:, -1, :]
    before = jnp.cumsum(totals, axis=0) - totals
    return (within + before[:, None, :]).reshape(count, width).astype(jnp.int32)


def select_rows(left, right, data, out_dtype):
    rows = left.shape[0]
    count, width = data.shape
    padded = -(-count // CHUNK) * CHUNK
    right = jnp.pad(right, (0, padded - count), constant_values=-1).reshape(1, padded)
    data = jnp.pad(data, ((0, padded - count), (0, 0)))
    block = _row_block(rows)
    return pl.pallas_call(
        functools.partial(_select_kernel, padded // CHUNK),
        out_shape=jax.ShapeDtypeStruct((rows, width), out_dtype),
        grid=(rows // block,),
        in_specs=[
            pl.BlockSpec((block, 1), lambda i: (i, 0)),
            pl.BlockSpec((1, padded), lambda i: (0, 0)),
            pl.BlockSpec((padded, width), lambda i: (0, 0)),
        ],
        out_specs=pl.BlockSpec((block, width), lambda i: (i, 0)),
        cost_estimate=pl.CostEstimate(
            flops=2 * rows * padded * width,
            transcendentals=0,
            bytes_accessed=padded * width * data.dtype.itemsize
            + rows * width * jnp.dtype(out_dtype).itemsize,
        ),
    )(left.reshape(rows, 1), right, data)


def local(
    bottom_out,
    owner_ids,
    row_ids,
    positions,
    labels,
    tables,
    cross_down,
    cross_up,
    cross_bias,
    out_weight,
    position_bias,
):
    sample_count, table_count = row_ids.shape
    rows_local = tables.shape[1]
    row_width = tables.shape[2]
    owner_count = lax.axis_size("emb")
    capacity = 3 * sample_count * table_count // (2 * owner_count)
    lookup_count = sample_count * table_count
    owners = owner_ids.reshape(sample_count, table_count)
    flat_owner = owners.reshape(-1)
    local_grid = jnp.arange(table_count, dtype=jnp.int32)[None, :] * rows_local + row_ids
    local_index = local_grid.reshape(-1)
    owner_marks = (flat_owner[:, None] == jnp.arange(owner_count, dtype=jnp.int32)[None, :]).astype(
        jnp.int32
    )
    ranking = _running_count(owner_marks) - 1
    slot_index = jnp.sum(ranking * owner_marks, axis=1)
    buffer_place = flat_owner * capacity + slot_index
    flat_table = tables.reshape(table_count * rows_local, row_width)
    request = jnp.zeros((owner_count * capacity,), jnp.int32).at[buffer_place].set(local_index)
    request = request.reshape(owner_count, capacity)
    received = lax.all_to_all(request, "emb", split_axis=0, concat_axis=0, tiled=True)
    slot_count = owner_count * capacity
    received_flat = received.reshape(-1)
    fetched = flat_table[received]
    arrived = lax.all_to_all(fetched, "emb", split_axis=0, concat_axis=0, tiled=True)
    pooled = arrived.reshape(slot_count, row_width)[buffer_place].reshape(
        sample_count, table_count * row_width
    )
    first = jnp.concatenate([bottom_out, pooled], axis=1)
    first_wide = first.astype(jnp.float32)
    weight_row = out_weight.astype(jnp.float32)
    reduced = jnp.dot(first, cross_down, preferred_element_type=jnp.float32).astype(jnp.bfloat16)
    gate_scale = jnp.dot(reduced, cross_up, preferred_element_type=jnp.float32) + cross_bias
    crossed = first_wide * gate_scale + first_wide
    position_marks = (
        positions[:, None] == jnp.arange(position_bias.shape[0], dtype=jnp.int32)[None, :]
    ).astype(jnp.float32)
    logit = jnp.sum(crossed * weight_row[None, :], axis=1) + jnp.sum(
        position_marks * position_bias[None, :], axis=1
    )
    err = jax.nn.sigmoid(logit) - labels.astype(jnp.float32)
    cotangent = err[:, None] * weight_row[None, :]
    scaled = cotangent * first_wide
    bias_local = jnp.sum(scaled, axis=0)
    device_count = lax.axis_size(("grp", "emb"))
    bias_parts = lax.all_to_all(
        jnp.broadcast_to(bias_local[None, :], (device_count, bias_local.shape[0])),
        ("grp", "emb"),
        split_axis=0,
        concat_axis=0,
        tiled=True,
    )
    down_grad = lax.dot_general(
        scaled.astype(jnp.bfloat16),
        cross_up,
        (((1,), (1,)), ((), ())),
        preferred_element_type=jnp.float32,
    ).astype(jnp.bfloat16)
    back_term = lax.dot_general(
        down_grad, cross_down, (((1,), (1,)), ((), ())), preferred_element_type=jnp.float32
    )
    input_grad = (cotangent * (gate_scale + 1.0) + back_term).astype(jnp.bfloat16)
    bottom_grad = input_grad[:, :row_width]
    row_grads = input_grad[:, row_width:].reshape(lookup_count, row_width)
    outgoing = jnp.zeros((slot_count, row_width), jnp.bfloat16).at[buffer_place].set(row_grads)
    incoming = lax.all_to_all(
        outgoing.reshape(owner_count, capacity, row_width),
        "emb",
        split_axis=0,
        concat_axis=0,
        tiled=True,
    )
    local_grad = select_rows(
        jnp.arange(table_count * rows_local, dtype=jnp.int32),
        received_flat,
        incoming.reshape(slot_count, row_width),
        jnp.float32,
    )
    summed_grad = lax.psum(local_grad.astype(jnp.bfloat16), "grp").astype(jnp.float32)
    table_grad = summed_grad.reshape(table_count, rows_local, row_width)
    bias_grad = jnp.sum(bias_parts, axis=0)
    return (table_grad, bottom_grad, bias_grad)


def solution(mesh):
    placed = (
        P(("grp", "emb"), None),
        P(("grp", "emb"), None),
        P(("grp", "emb"), None),
        P(("grp", "emb")),
        P(("grp", "emb")),
        P(None, "emb", None),
        P(),
        P(),
        P(),
        P(),
        P(),
    )
    return jax.shard_map(
        local,
        mesh=mesh,
        in_specs=placed,
        out_specs=(P(None, "emb", None), P(("grp", "emb"), None), P()),
        check_vma=False,
    )
```

```python
import functools

import jax
import jax.numpy as jnp
from jax import lax
from jax.experimental import pallas as pl
from jax.experimental.pallas import tpu as pltpu
from jax.sharding import PartitionSpec as P

CHUNK = 512


def _row_block(rows):
    if rows <= 4096:
        return rows
    for size in range(4096, 7, -8):
        if rows % size == 0:
            return size
    return rows


def _select_kernel(chunks, left_ref, right_ref, data_ref, out_ref):
    left = left_ref[...]

    def step(j, acc):
        start = pl.multiple_of(j * CHUNK, CHUNK)
        right = right_ref[:, pl.ds(start, CHUNK)]
        picks = jnp.where(left == right, 1.0, 0.0).astype(data_ref.dtype)
        block = data_ref[pl.ds(start, CHUNK), :]
        return acc + jnp.dot(picks, block, preferred_element_type=jnp.float32)

    acc = jnp.zeros(out_ref.shape, jnp.float32)
    acc = lax.fori_loop(0, chunks, step, acc)
    out_ref[...] = acc.astype(out_ref.dtype)


def _running_count(marks):
    count, width = marks.shape
    block = 128 if count % 128 == 0 else count
    grouped = marks.reshape(count // block, block, width).astype(jnp.bfloat16)
    lower = (
        jnp.arange(block, dtype=jnp.int32)[:, None] >= jnp.arange(block, dtype=jnp.int32)[None, :]
    ).astype(jnp.bfloat16)
    within = jnp.einsum("rc,bcj->brj", lower, grouped, preferred_element_type=jnp.float32)
    totals = within[:, -1, :]
    before = jnp.cumsum(totals, axis=0) - totals
    return (within + before[:, None, :]).reshape(count, width).astype(jnp.int32)


def select_rows(left, right, data, out_dtype):
    rows = left.shape[0]
    count, width = data.shape
    padded = -(-count // CHUNK) * CHUNK
    right = jnp.pad(right, (0, padded - count), constant_values=-1).reshape(1, padded)
    data = jnp.pad(data, ((0, padded - count), (0, 0)))
    block = _row_block(rows)
    return pl.pallas_call(
        functools.partial(_select_kernel, padded // CHUNK),
        out_shape=jax.ShapeDtypeStruct((rows, width), out_dtype),
        grid=(rows // block,),
        in_specs=[
            pl.BlockSpec((block, 1), lambda i: (i, 0)),
            pl.BlockSpec((1, padded), lambda i: (0, 0)),
            pl.BlockSpec((padded, width), lambda i: (0, 0)),
        ],
        out_specs=pl.BlockSpec((block, width), lambda i: (i, 0)),
        cost_estimate=pl.CostEstimate(
            flops=2 * rows * padded * width,
            transcendentals=0,
            bytes_accessed=padded * width * data.dtype.itemsize
            + rows * width * jnp.dtype(out_dtype).itemsize,
        ),
    )(left.reshape(rows, 1), right, data)


def local(
    bottom_out,
    owner_ids,
    row_ids,
    positions,
    labels,
    tables,
    cross_down,
    cross_up,
    cross_bias,
    out_weight,
    position_bias,
):
    sample_count, table_count = row_ids.shape
    rows_local = tables.shape[1]
    row_width = tables.shape[2]
    owner_count = lax.axis_size("emb")
    capacity = 3 * sample_count * table_count // (2 * owner_count)
    lookup_count = sample_count * table_count
    owners = owner_ids.reshape(sample_count, table_count)
    flat_owner = owners.reshape(-1)
    local_grid = jnp.arange(table_count, dtype=jnp.int32)[None, :] * rows_local + row_ids
    local_index = local_grid.reshape(-1)
    owner_marks = (flat_owner[:, None] == jnp.arange(owner_count, dtype=jnp.int32)[None, :]).astype(
        jnp.int32
    )
    ranking = _running_count(owner_marks) - 1
    slot_index = jnp.sum(ranking * owner_marks, axis=1)
    buffer_place = flat_owner * capacity + slot_index
    flat_table = tables.reshape(table_count * rows_local, row_width)
    request = jnp.zeros((owner_count * capacity,), jnp.int32).at[buffer_place].set(local_index)
    request = request.reshape(owner_count, capacity)
    received = lax.all_to_all(request, "emb", split_axis=0, concat_axis=0, tiled=True)
    slot_count = owner_count * capacity
    received_flat = received.reshape(-1)
    fetched = flat_table[received]
    arrived = lax.all_to_all(fetched, "emb", split_axis=0, concat_axis=0, tiled=True)
    pooled = arrived.reshape(slot_count, row_width)[buffer_place].reshape(
        sample_count, table_count * row_width
    )
    first = jnp.concatenate([bottom_out, pooled], axis=1)
    first_wide = first.astype(jnp.float32)
    weight_row = out_weight.astype(jnp.float32)
    reduced = jnp.dot(first, cross_down, preferred_element_type=jnp.float32).astype(jnp.bfloat16)
    gate_scale = jnp.dot(reduced, cross_up, preferred_element_type=jnp.float32) + cross_bias
    crossed = first_wide * gate_scale + first_wide
    position_marks = (
        positions[:, None] == jnp.arange(position_bias.shape[0], dtype=jnp.int32)[None, :]
    ).astype(jnp.float32)
    logit = jnp.sum(crossed * weight_row[None, :], axis=1) + jnp.sum(
        position_marks * position_bias[None, :], axis=1
    )
    err = jax.nn.sigmoid(logit) - labels.astype(jnp.float32)
    cotangent = err[:, None] * weight_row[None, :]
    scaled = cotangent * first_wide
    bias_local = jnp.sum(scaled, axis=0)
    device_count = lax.axis_size(("grp", "emb"))
    bias_parts = lax.all_to_all(
        jnp.broadcast_to(bias_local[None, :], (device_count, bias_local.shape[0])),
        ("grp", "emb"),
        split_axis=0,
        concat_axis=0,
        tiled=True,
    )
    down_grad = lax.dot_general(
        scaled.astype(jnp.bfloat16),
        cross_up,
        (((1,), (1,)), ((), ())),
        preferred_element_type=jnp.float32,
    ).astype(jnp.bfloat16)
    back_term = lax.dot_general(
        down_grad, cross_down, (((1,), (1,)), ((), ())), preferred_element_type=jnp.float32
    )
    input_grad = (cotangent * (gate_scale + 1.0) + back_term).astype(jnp.bfloat16)
    bottom_grad = input_grad[:, :row_width]
    row_grads = input_grad[:, row_width:].reshape(lookup_count, row_width)
    outgoing = jnp.zeros((slot_count, row_width), jnp.bfloat16).at[buffer_place].set(row_grads)
    incoming = lax.all_to_all(
        outgoing.reshape(owner_count, capacity, row_width),
        "emb",
        split_axis=0,
        concat_axis=0,
        tiled=True,
    )
    local_grad = select_rows(
        jnp.arange(table_count * rows_local, dtype=jnp.int32),
        received_flat,
        incoming.reshape(slot_count, row_width),
        jnp.float32,
    )
    copies = lax.axis_size("grp")
    part_rows = local_grad.shape[0] // copies
    parts = local_grad.astype(jnp.bfloat16).reshape(copies, part_rows, row_width)
    parts = lax.all_to_all(parts, "grp", split_axis=0, concat_axis=0, tiled=True)
    owned = jnp.sum(parts.astype(jnp.float32), axis=0).astype(jnp.bfloat16)
    spread = jnp.broadcast_to(owned[None], (copies, part_rows, row_width))
    spread = lax.all_to_all(spread, "grp", split_axis=0, concat_axis=0, tiled=True)
    summed_grad = spread.reshape(copies * part_rows, row_width).astype(jnp.float32)
    table_grad = summed_grad.reshape(table_count, rows_local, row_width)
    bias_grad = jnp.sum(bias_parts, axis=0)
    return (table_grad, bottom_grad, bias_grad)


def solution(mesh):
    placed = (
        P(("grp", "emb"), None),
        P(("grp", "emb"), None),
        P(("grp", "emb"), None),
        P(("grp", "emb")),
        P(("grp", "emb")),
        P(None, "emb", None),
        P(),
        P(),
        P(),
        P(),
        P(),
    )
    return jax.shard_map(
        local,
        mesh=mesh,
        in_specs=placed,
        out_specs=(P(None, "emb", None), P(("grp", "emb"), None), P()),
        check_vma=False,
    )
```

```python
import functools

import jax
import jax.numpy as jnp
from jax import lax
from jax.experimental import pallas as pl
from jax.experimental.pallas import tpu as pltpu
from jax.sharding import PartitionSpec as P

CHUNK = 512


def _row_block(rows):
    if rows <= 4096:
        return rows
    for size in range(4096, 7, -8):
        if rows % size == 0:
            return size
    return rows


def _select_kernel(chunks, left_ref, right_ref, data_ref, out_ref):
    left = left_ref[...]

    def step(j, acc):
        start = pl.multiple_of(j * CHUNK, CHUNK)
        right = right_ref[:, pl.ds(start, CHUNK)]
        picks = jnp.where(left == right, 1.0, 0.0).astype(data_ref.dtype)
        block = data_ref[pl.ds(start, CHUNK), :]
        return acc + jnp.dot(picks, block, preferred_element_type=jnp.float32)

    acc = jnp.zeros(out_ref.shape, jnp.float32)
    acc = lax.fori_loop(0, chunks, step, acc)
    out_ref[...] = acc.astype(out_ref.dtype)


def _running_count(marks):
    count, width = marks.shape
    block = 128 if count % 128 == 0 else count
    grouped = marks.reshape(count // block, block, width).astype(jnp.bfloat16)
    lower = (
        jnp.arange(block, dtype=jnp.int32)[:, None] >= jnp.arange(block, dtype=jnp.int32)[None, :]
    ).astype(jnp.bfloat16)
    within = jnp.einsum("rc,bcj->brj", lower, grouped, preferred_element_type=jnp.float32)
    totals = within[:, -1, :]
    before = jnp.cumsum(totals, axis=0) - totals
    return (within + before[:, None, :]).reshape(count, width).astype(jnp.int32)


def _in_thirds(values, width):
    high = values.astype(jnp.bfloat16)
    rest = values - high.astype(jnp.float32)
    middle = rest.astype(jnp.bfloat16)
    low = (rest - middle.astype(jnp.float32)).astype(jnp.bfloat16)
    return jnp.stack([high, middle, low]).reshape(-1, width)


def _from_thirds(rows, count):
    return jnp.sum(rows.astype(jnp.float32).reshape(-1, 3, count), axis=(0, 1))


def select_rows(left, right, data, out_dtype):
    rows = left.shape[0]
    count, width = data.shape
    padded = -(-count // CHUNK) * CHUNK
    right = jnp.pad(right, (0, padded - count), constant_values=-1).reshape(1, padded)
    data = jnp.pad(data, ((0, padded - count), (0, 0)))
    block = _row_block(rows)
    return pl.pallas_call(
        functools.partial(_select_kernel, padded // CHUNK),
        out_shape=jax.ShapeDtypeStruct((rows, width), out_dtype),
        grid=(rows // block,),
        in_specs=[
            pl.BlockSpec((block, 1), lambda i: (i, 0)),
            pl.BlockSpec((1, padded), lambda i: (0, 0)),
            pl.BlockSpec((padded, width), lambda i: (0, 0)),
        ],
        out_specs=pl.BlockSpec((block, width), lambda i: (i, 0)),
        cost_estimate=pl.CostEstimate(
            flops=2 * rows * padded * width,
            transcendentals=0,
            bytes_accessed=padded * width * data.dtype.itemsize
            + rows * width * jnp.dtype(out_dtype).itemsize,
        ),
    )(left.reshape(rows, 1), right, data)


def local(
    bottom_out,
    owner_ids,
    row_ids,
    positions,
    labels,
    tables,
    cross_down,
    cross_up,
    cross_bias,
    out_weight,
    position_bias,
):
    sample_count, table_count = row_ids.shape
    rows_local = tables.shape[1]
    row_width = tables.shape[2]
    owner_count = lax.axis_size("emb")
    capacity = 3 * sample_count * table_count // (2 * owner_count)
    lookup_count = sample_count * table_count
    owners = owner_ids.reshape(sample_count, table_count)
    flat_owner = owners.reshape(-1)
    local_grid = jnp.arange(table_count, dtype=jnp.int32)[None, :] * rows_local + row_ids
    local_index = local_grid.reshape(-1)
    owner_marks = (flat_owner[:, None] == jnp.arange(owner_count, dtype=jnp.int32)[None, :]).astype(
        jnp.int32
    )
    ranking = _running_count(owner_marks) - 1
    slot_index = jnp.sum(ranking * owner_marks, axis=1)
    buffer_place = flat_owner * capacity + slot_index
    flat_table = tables.reshape(table_count * rows_local, row_width)
    request = jnp.zeros((owner_count * capacity,), jnp.int32).at[buffer_place].set(local_index)
    request = request.reshape(owner_count, capacity)
    received = lax.all_to_all(request, "emb", split_axis=0, concat_axis=0, tiled=True)
    slot_count = owner_count * capacity
    received_flat = received.reshape(-1)
    fetched = flat_table[received]
    arrived = lax.all_to_all(fetched, "emb", split_axis=0, concat_axis=0, tiled=True)
    pooled = arrived.reshape(slot_count, row_width)[buffer_place].reshape(
        sample_count, table_count * row_width
    )
    first = jnp.concatenate([bottom_out, pooled], axis=1)
    first_wide = first.astype(jnp.float32)
    weight_row = out_weight.astype(jnp.float32)
    reduced = jnp.dot(first, cross_down, preferred_element_type=jnp.float32).astype(jnp.bfloat16)
    gate_scale = jnp.dot(reduced, cross_up, preferred_element_type=jnp.float32) + cross_bias
    crossed = first_wide * gate_scale + first_wide
    position_marks = (
        positions[:, None] == jnp.arange(position_bias.shape[0], dtype=jnp.int32)[None, :]
    ).astype(jnp.float32)
    logit = jnp.sum(crossed * weight_row[None, :], axis=1) + jnp.sum(
        position_marks * position_bias[None, :], axis=1
    )
    err = jax.nn.sigmoid(logit) - labels.astype(jnp.float32)
    cotangent = err[:, None] * weight_row[None, :]
    scaled = cotangent * first_wide
    bias_rows = _in_thirds(jnp.sum(scaled, axis=0), row_width)
    bias_count = bias_rows.shape[0]
    down_grad = lax.dot_general(
        scaled.astype(jnp.bfloat16),
        cross_up,
        (((1,), (1,)), ((), ())),
        preferred_element_type=jnp.float32,
    ).astype(jnp.bfloat16)
    back_term = lax.dot_general(
        down_grad, cross_down, (((1,), (1,)), ((), ())), preferred_element_type=jnp.float32
    )
    input_grad = (cotangent * (gate_scale + 1.0) + back_term).astype(jnp.bfloat16)
    bottom_grad = input_grad[:, :row_width]
    row_grads = input_grad[:, row_width:].reshape(lookup_count, row_width)
    outgoing = jnp.zeros((slot_count, row_width), jnp.bfloat16).at[buffer_place].set(row_grads)
    outgoing = jnp.concatenate(
        [
            outgoing.reshape(owner_count, capacity, row_width),
            jnp.broadcast_to(bias_rows[None], (owner_count, bias_count, row_width)),
        ],
        axis=1,
    )
    incoming = lax.all_to_all(outgoing, "emb", split_axis=0, concat_axis=0, tiled=True)
    bias_emb = _from_thirds(incoming[:, capacity:], scaled.shape[1])
    incoming = incoming[:, :capacity]
    local_grad = select_rows(
        jnp.arange(table_count * rows_local, dtype=jnp.int32),
        received_flat,
        incoming.reshape(slot_count, row_width),
        jnp.float32,
    )
    copies = lax.axis_size("grp")
    payload = jnp.concatenate(
        [local_grad.astype(jnp.bfloat16), _in_thirds(bias_emb, row_width)], axis=0
    )
    spread = lax.all_to_all(
        jnp.broadcast_to(payload[None], (copies,) + payload.shape),
        "grp",
        split_axis=0,
        concat_axis=0,
        tiled=True,
    )
    grad_rows = local_grad.shape[0]
    table_grad = jnp.sum(spread[:, :grad_rows].astype(jnp.float32), axis=0).reshape(
        table_count, rows_local, row_width
    )
    bias_grad = _from_thirds(spread[:, grad_rows:], scaled.shape[1])
    return (table_grad, bottom_grad, bias_grad)


def solution(mesh):
    placed = (
        P(("grp", "emb"), None),
        P(("grp", "emb"), None),
        P(("grp", "emb"), None),
        P(("grp", "emb")),
        P(("grp", "emb")),
        P(None, "emb", None),
        P(),
        P(),
        P(),
        P(),
        P(),
    )
    return jax.shard_map(
        local,
        mesh=mesh,
        in_specs=placed,
        out_specs=(P(None, "emb", None), P(("grp", "emb"), None), P()),
        check_vma=False,
    )
```

```python
import functools

import jax
import jax.numpy as jnp
from jax import lax
from jax.experimental import pallas as pl
from jax.experimental.pallas import tpu as pltpu
from jax.sharding import PartitionSpec as P

CHUNK = 512


def _row_block(rows):
    if rows <= 4096:
        return rows
    for size in range(4096, 7, -8):
        if rows % size == 0:
            return size
    return rows


def _select_kernel(chunks, left_ref, right_ref, data_ref, out_ref):
    left = left_ref[...]

    def step(j, acc):
        start = pl.multiple_of(j * CHUNK, CHUNK)
        right = right_ref[:, pl.ds(start, CHUNK)]
        picks = jnp.where(left == right, 1.0, 0.0).astype(data_ref.dtype)
        block = data_ref[pl.ds(start, CHUNK), :]
        return acc + jnp.dot(picks, block, preferred_element_type=jnp.float32)

    acc = jnp.zeros(out_ref.shape, jnp.float32)
    acc = lax.fori_loop(0, chunks, step, acc)
    out_ref[...] = acc.astype(out_ref.dtype)


def _running_count(marks):
    count, width = marks.shape
    block = 128 if count % 128 == 0 else count
    grouped = marks.reshape(count // block, block, width).astype(jnp.bfloat16)
    lower = (
        jnp.arange(block, dtype=jnp.int32)[:, None] >= jnp.arange(block, dtype=jnp.int32)[None, :]
    ).astype(jnp.bfloat16)
    within = jnp.einsum("rc,bcj->brj", lower, grouped, preferred_element_type=jnp.float32)
    totals = within[:, -1, :]
    before = jnp.cumsum(totals, axis=0) - totals
    return (within + before[:, None, :]).reshape(count, width).astype(jnp.int32)


def _in_thirds(values, width):
    high = values.astype(jnp.bfloat16)
    rest = values - high.astype(jnp.float32)
    middle = rest.astype(jnp.bfloat16)
    low = (rest - middle.astype(jnp.float32)).astype(jnp.bfloat16)
    return jnp.stack([high, middle, low]).reshape(-1, width)


def _from_thirds(rows, count):
    return jnp.sum(rows.astype(jnp.float32).reshape(-1, 3, count), axis=(0, 1))


def select_rows(left, right, data, out_dtype):
    rows = left.shape[0]
    count, width = data.shape
    padded = -(-count // CHUNK) * CHUNK
    right = jnp.pad(right, (0, padded - count), constant_values=-1).reshape(1, padded)
    data = jnp.pad(data, ((0, padded - count), (0, 0)))
    block = _row_block(rows)
    return pl.pallas_call(
        functools.partial(_select_kernel, padded // CHUNK),
        out_shape=jax.ShapeDtypeStruct((rows, width), out_dtype),
        grid=(rows // block,),
        in_specs=[
            pl.BlockSpec((block, 1), lambda i: (i, 0)),
            pl.BlockSpec((1, padded), lambda i: (0, 0)),
            pl.BlockSpec((padded, width), lambda i: (0, 0)),
        ],
        out_specs=pl.BlockSpec((block, width), lambda i: (i, 0)),
        cost_estimate=pl.CostEstimate(
            flops=2 * rows * padded * width,
            transcendentals=0,
            bytes_accessed=padded * width * data.dtype.itemsize
            + rows * width * jnp.dtype(out_dtype).itemsize,
        ),
    )(left.reshape(rows, 1), right, data)


def local(
    bottom_out,
    owner_ids,
    row_ids,
    positions,
    labels,
    tables,
    cross_down,
    cross_up,
    cross_bias,
    out_weight,
    position_bias,
):
    sample_count, table_count = row_ids.shape
    rows_local = tables.shape[1]
    row_width = tables.shape[2]
    owner_count = lax.axis_size("emb")
    capacity = 3 * sample_count * table_count // (2 * owner_count)
    lookup_count = sample_count * table_count
    owners = owner_ids.reshape(sample_count, table_count)
    flat_owner = owners.reshape(-1)
    local_grid = jnp.arange(table_count, dtype=jnp.int32)[None, :] * rows_local + row_ids
    local_index = local_grid.reshape(-1)
    owner_marks = (flat_owner[:, None] == jnp.arange(owner_count, dtype=jnp.int32)[None, :]).astype(
        jnp.int32
    )
    ranking = _running_count(owner_marks) - 1
    slot_index = jnp.sum(ranking * owner_marks, axis=1)
    buffer_place = flat_owner * capacity + slot_index
    flat_table = tables.reshape(table_count * rows_local, row_width)
    request = jnp.zeros((owner_count * capacity,), jnp.int32).at[buffer_place].set(local_index)
    request = request.reshape(owner_count, capacity)
    received = lax.all_to_all(request, "emb", split_axis=0, concat_axis=0, tiled=True)
    slot_count = owner_count * capacity
    received_flat = received.reshape(-1)
    fetched = flat_table[received]
    arrived = lax.all_to_all(fetched, "emb", split_axis=0, concat_axis=0, tiled=True)
    pooled = arrived.reshape(slot_count, row_width)[buffer_place].reshape(
        sample_count, table_count * row_width
    )
    first = jnp.concatenate([bottom_out, pooled], axis=1)
    first_wide = first.astype(jnp.float32)
    weight_row = out_weight.astype(jnp.float32)
    reduced = jnp.dot(first, cross_down, preferred_element_type=jnp.float32).astype(jnp.bfloat16)
    gate_scale = jnp.dot(reduced, cross_up, preferred_element_type=jnp.float32) + cross_bias
    crossed = first_wide * gate_scale + first_wide
    position_marks = (
        positions[:, None] == jnp.arange(position_bias.shape[0], dtype=jnp.int32)[None, :]
    ).astype(jnp.float32)
    logit = jnp.sum(crossed * weight_row[None, :], axis=1) + jnp.sum(
        position_marks * position_bias[None, :], axis=1
    )
    err = jax.nn.sigmoid(logit) - labels.astype(jnp.float32)
    cotangent = err[:, None] * weight_row[None, :]
    scaled = cotangent * first_wide
    bias_rows = _in_thirds(jnp.sum(scaled, axis=0), row_width)
    bias_count = bias_rows.shape[0]
    down_grad = lax.dot_general(
        scaled.astype(jnp.bfloat16),
        cross_up,
        (((1,), (1,)), ((), ())),
        preferred_element_type=jnp.float32,
    ).astype(jnp.bfloat16)
    back_term = lax.dot_general(
        down_grad, cross_down, (((1,), (1,)), ((), ())), preferred_element_type=jnp.float32
    )
    input_grad = (cotangent * (gate_scale + 1.0) + back_term).astype(jnp.bfloat16)
    bottom_grad = input_grad[:, :row_width]
    row_grads = input_grad[:, row_width:].reshape(lookup_count, row_width)
    outgoing = jnp.zeros((slot_count, row_width), jnp.bfloat16).at[buffer_place].set(row_grads)
    outgoing = jnp.concatenate(
        [
            outgoing.reshape(owner_count, capacity, row_width),
            jnp.broadcast_to(bias_rows[None], (owner_count, bias_count, row_width)),
        ],
        axis=1,
    )
    incoming = lax.all_to_all(outgoing, "emb", split_axis=0, concat_axis=0, tiled=True)
    bias_emb = _from_thirds(incoming[:, capacity:], scaled.shape[1])
    incoming = incoming[:, :capacity]
    local_grad = select_rows(
        jnp.arange(table_count * rows_local, dtype=jnp.int32),
        received_flat,
        incoming.reshape(slot_count, row_width),
        jnp.float32,
    )
    copies = lax.axis_size("grp")
    part_rows = local_grad.shape[0] // copies
    bias_thirds = _in_thirds(bias_emb, row_width)
    parts = jnp.concatenate(
        [
            local_grad.astype(jnp.bfloat16).reshape(copies, part_rows, row_width),
            jnp.broadcast_to(bias_thirds[None], (copies,) + bias_thirds.shape),
        ],
        axis=1,
    )
    parts = lax.all_to_all(parts, "grp", split_axis=0, concat_axis=0, tiled=True)
    bias_grad = _from_thirds(parts[:, part_rows:], scaled.shape[1])
    owned = jnp.sum(parts[:, :part_rows].astype(jnp.float32), axis=0).astype(jnp.bfloat16)
    spread = lax.all_to_all(
        jnp.broadcast_to(owned[None], (copies, part_rows, row_width)),
        "grp",
        split_axis=0,
        concat_axis=0,
        tiled=True,
    )
    table_grad = spread.astype(jnp.float32).reshape(table_count, rows_local, row_width)
    return (table_grad, bottom_grad, bias_grad)


def solution(mesh):
    placed = (
        P(("grp", "emb"), None),
        P(("grp", "emb"), None),
        P(("grp", "emb"), None),
        P(("grp", "emb")),
        P(("grp", "emb")),
        P(None, "emb", None),
        P(),
        P(),
        P(),
        P(),
        P(),
    )
    return jax.shard_map(
        local,
        mesh=mesh,
        in_specs=placed,
        out_specs=(P(None, "emb", None), P(("grp", "emb"), None), P()),
        check_vma=False,
    )
```

```python
import functools

import jax
import jax.numpy as jnp
from jax import lax
from jax.experimental import pallas as pl
from jax.experimental.pallas import tpu as pltpu
from jax.sharding import PartitionSpec as P

CHUNK = 512


def _row_block(rows):
    if rows <= 4096:
        return rows
    for size in range(4096, 7, -8):
        if rows % size == 0:
            return size
    return rows


def _select_kernel(chunks, left_ref, right_ref, data_ref, out_ref):
    left = left_ref[...]

    def step(j, acc):
        start = pl.multiple_of(j * CHUNK, CHUNK)
        right = right_ref[:, pl.ds(start, CHUNK)]
        picks = jnp.where(left == right, 1.0, 0.0).astype(data_ref.dtype)
        block = data_ref[pl.ds(start, CHUNK), :]
        return acc + jnp.dot(picks, block, preferred_element_type=jnp.float32)

    acc = jnp.zeros(out_ref.shape, jnp.float32)
    acc = lax.fori_loop(0, chunks, step, acc)
    out_ref[...] = acc.astype(out_ref.dtype)


def select_rows(left, right, data, out_dtype):
    rows = left.shape[0]
    count, width = data.shape
    padded = -(-count // CHUNK) * CHUNK
    right = jnp.pad(right, (0, padded - count), constant_values=-1).reshape(1, padded)
    data = jnp.pad(data, ((0, padded - count), (0, 0)))
    block = _row_block(rows)
    return pl.pallas_call(
        functools.partial(_select_kernel, padded // CHUNK),
        out_shape=jax.ShapeDtypeStruct((rows, width), out_dtype),
        grid=(rows // block,),
        in_specs=[
            pl.BlockSpec((block, 1), lambda i: (i, 0)),
            pl.BlockSpec((1, padded), lambda i: (0, 0)),
            pl.BlockSpec((padded, width), lambda i: (0, 0)),
        ],
        out_specs=pl.BlockSpec((block, width), lambda i: (i, 0)),
        cost_estimate=pl.CostEstimate(
            flops=2 * rows * padded * width,
            transcendentals=0,
            bytes_accessed=padded * width * data.dtype.itemsize
            + rows * width * jnp.dtype(out_dtype).itemsize,
        ),
    )(left.reshape(rows, 1), right, data)


def local(
    bottom_out,
    owner_ids,
    row_ids,
    positions,
    labels,
    tables,
    cross_down,
    cross_up,
    cross_bias,
    out_weight,
    position_bias,
):
    sample_count, table_count = row_ids.shape
    rows_local = tables.shape[1]
    row_width = tables.shape[2]
    owner_count = lax.axis_size("emb")
    capacity = 3 * sample_count * table_count // (2 * owner_count)
    lookup_count = sample_count * table_count
    owners = owner_ids.reshape(sample_count, table_count)
    flat_owner = owners.reshape(-1)
    local_grid = jnp.arange(table_count, dtype=jnp.int32)[None, :] * rows_local + row_ids
    local_index = local_grid.reshape(-1)
    owner_marks = (flat_owner[:, None] == jnp.arange(owner_count, dtype=jnp.int32)[None, :]).astype(
        jnp.int32
    )
    ranking = jnp.cumsum(owner_marks, axis=0) - 1
    slot_index = jnp.sum(ranking * owner_marks, axis=1)
    buffer_place = flat_owner * capacity + slot_index
    flat_table = tables.reshape(table_count * rows_local, row_width)
    request = jnp.zeros((owner_count * capacity,), jnp.int32).at[buffer_place].set(local_index)
    request = request.reshape(owner_count, capacity)
    received = lax.all_to_all(request, "emb", split_axis=0, concat_axis=0, tiled=True)
    slot_count = owner_count * capacity
    received_flat = received.reshape(-1)
    fetched = flat_table[received]
    arrived = lax.all_to_all(fetched, "emb", split_axis=0, concat_axis=0, tiled=True)
    pooled = arrived.reshape(slot_count, row_width)[buffer_place].reshape(
        sample_count, table_count * row_width
    )
    first = jnp.concatenate([bottom_out, pooled], axis=1)
    first_wide = first.astype(jnp.float32)
    weight_row = out_weight.astype(jnp.float32)
    reduced = jnp.dot(first, cross_down, preferred_element_type=jnp.float32).astype(jnp.bfloat16)
    gate_scale = jnp.dot(reduced, cross_up, preferred_element_type=jnp.float32) + cross_bias
    crossed = first_wide * gate_scale + first_wide
    position_marks = (
        positions[:, None] == jnp.arange(position_bias.shape[0], dtype=jnp.int32)[None, :]
    ).astype(jnp.float32)
    logit = jnp.sum(crossed * weight_row[None, :], axis=1) + jnp.sum(
        position_marks * position_bias[None, :], axis=1
    )
    err = jax.nn.sigmoid(logit) - labels.astype(jnp.float32)
    cotangent = err[:, None] * weight_row[None, :]
    scaled = cotangent * first_wide
    down_grad = lax.dot_general(
        scaled.astype(jnp.bfloat16),
        cross_up,
        (((1,), (1,)), ((), ())),
        preferred_element_type=jnp.float32,
    ).astype(jnp.bfloat16)
    back_term = lax.dot_general(
        down_grad, cross_down, (((1,), (1,)), ((), ())), preferred_element_type=jnp.float32
    )
    input_grad = (cotangent * (gate_scale + 1.0) + back_term).astype(jnp.bfloat16)
    bottom_grad = input_grad[:, :row_width]
    row_grads = input_grad[:, row_width:].reshape(lookup_count, row_width)
    outgoing = jnp.zeros((slot_count, row_width), jnp.bfloat16).at[buffer_place].set(row_grads)
    incoming = lax.all_to_all(
        outgoing.reshape(owner_count, capacity, row_width),
        "emb",
        split_axis=0,
        concat_axis=0,
        tiled=True,
    )
    local_grad = select_rows(
        jnp.arange(table_count * rows_local, dtype=jnp.int32),
        received_flat,
        incoming.reshape(slot_count, row_width),
        jnp.float32,
    )
    summed_grad = lax.psum(local_grad.astype(jnp.bfloat16), "grp").astype(jnp.float32)
    table_grad = summed_grad.reshape(table_count, rows_local, row_width)
    bias_local = jnp.sum(scaled, axis=0)
    bias_grad = lax.psum(bias_local, ("grp", "emb"))
    return (table_grad, bottom_grad, bias_grad)


def solution(mesh):
    placed = (
        P(("grp", "emb"), None),
        P(("grp", "emb"), None),
        P(("grp", "emb"), None),
        P(("grp", "emb")),
        P(("grp", "emb")),
        P(None, "emb", None),
        P(),
        P(),
        P(),
        P(),
        P(),
    )
    return jax.shard_map(
        local,
        mesh=mesh,
        in_specs=placed,
        out_specs=(P(None, "emb", None), P(("grp", "emb"), None), P()),
        check_vma=False,
    )
```

```python
import functools

import jax
import jax.numpy as jnp
from jax import lax
from jax.experimental import pallas as pl
from jax.experimental.pallas import tpu as pltpu
from jax.sharding import PartitionSpec as P

def _row_block(rows):
    if rows <= 4096:
        return rows
    for size in range(4096, 7, -8):
        if rows % size == 0:
            return size
    return rows


def _chunk_of(count):
    for size in (512, 384, 256, 128):
        if count % size == 0:
            return size
    return 512


def _select_kernel(chunk, chunks, right_ref, data_ref, out_ref):
    block = out_ref.shape[0]
    left = lax.broadcasted_iota(jnp.int32, (block, 1), 0) + pl.program_id(0) * block

    def step(j, acc):
        start = pl.multiple_of(j * chunk, chunk)
        right = right_ref[:, pl.ds(start, chunk)]
        picks = jnp.where(left == right, 1.0, 0.0).astype(data_ref.dtype)
        part = data_ref[pl.ds(start, chunk), :]
        return acc + jnp.dot(picks, part, preferred_element_type=jnp.float32)

    acc = jnp.zeros(out_ref.shape, jnp.float32)
    acc = lax.fori_loop(0, chunks, step, acc)
    out_ref[...] = acc.astype(out_ref.dtype)


def add_rows(rows, right, data, out_dtype):
    count, width = data.shape
    chunk = _chunk_of(count)
    padded = -(-count // chunk) * chunk
    if padded != count:
        right = jnp.pad(right, (0, padded - count), constant_values=-1)
        data = jnp.pad(data, ((0, padded - count), (0, 0)))
    right = right.reshape(1, padded)
    block = _row_block(rows)
    return pl.pallas_call(
        functools.partial(_select_kernel, chunk, padded // chunk),
        out_shape=jax.ShapeDtypeStruct((rows, width), out_dtype),
        grid=(rows // block,),
        in_specs=[
            pl.BlockSpec((1, padded), lambda i: (0, 0)),
            pl.BlockSpec((padded, width), lambda i: (0, 0)),
        ],
        out_specs=pl.BlockSpec((block, width), lambda i: (i, 0)),
        cost_estimate=pl.CostEstimate(
            flops=2 * rows * padded * width,
            transcendentals=0,
            bytes_accessed=padded * width * data.dtype.itemsize
            + rows * width * jnp.dtype(out_dtype).itemsize,
        ),
    )(right, data)


def local(
    bottom_out,
    owner_ids,
    row_ids,
    positions,
    labels,
    tables,
    cross_down,
    cross_up,
    cross_bias,
    out_weight,
    position_bias,
):
    sample_count, table_count = row_ids.shape
    rows_local = tables.shape[1]
    row_width = tables.shape[2]
    owner_count = lax.axis_size("emb")
    capacity = 3 * sample_count * table_count // (2 * owner_count)
    lookup_count = sample_count * table_count
    owners = owner_ids.reshape(sample_count, table_count)
    flat_owner = owners.reshape(-1)
    local_grid = jnp.arange(table_count, dtype=jnp.int32)[None, :] * rows_local + row_ids
    local_index = local_grid.reshape(-1)
    owner_marks = (flat_owner[:, None] == jnp.arange(owner_count, dtype=jnp.int32)[None, :]).astype(
        jnp.int32
    )
    ranking = jnp.cumsum(owner_marks, axis=0) - 1
    slot_index = jnp.sum(ranking * owner_marks, axis=1)
    buffer_place = flat_owner * capacity + slot_index
    flat_table = tables.reshape(table_count * rows_local, row_width)
    request = jnp.zeros((owner_count * capacity,), jnp.int32).at[buffer_place].set(local_index)
    request = request.reshape(owner_count, capacity)
    received = lax.all_to_all(request, "emb", split_axis=0, concat_axis=0, tiled=True)
    slot_count = owner_count * capacity
    received_flat = received.reshape(-1)
    fetched = flat_table[received]
    arrived = lax.all_to_all(fetched, "emb", split_axis=0, concat_axis=0, tiled=True)
    pooled = arrived.reshape(slot_count, row_width)[buffer_place].reshape(
        sample_count, table_count * row_width
    )
    first = jnp.concatenate([bottom_out, pooled], axis=1)
    first_wide = first.astype(jnp.float32)
    weight_row = out_weight.astype(jnp.float32)
    reduced = jnp.dot(first, cross_down, preferred_element_type=jnp.float32).astype(jnp.bfloat16)
    gate_scale = jnp.dot(reduced, cross_up, preferred_element_type=jnp.float32) + cross_bias
    crossed = first_wide * gate_scale + first_wide
    position_marks = (
        positions[:, None] == jnp.arange(position_bias.shape[0], dtype=jnp.int32)[None, :]
    ).astype(jnp.float32)
    logit = jnp.sum(crossed * weight_row[None, :], axis=1) + jnp.sum(
        position_marks * position_bias[None, :], axis=1
    )
    err = jax.nn.sigmoid(logit) - labels.astype(jnp.float32)
    cotangent = err[:, None] * weight_row[None, :]
    scaled = cotangent * first_wide
    down_grad = lax.dot_general(
        scaled.astype(jnp.bfloat16),
        cross_up,
        (((1,), (1,)), ((), ())),
        preferred_element_type=jnp.float32,
    ).astype(jnp.bfloat16)
    back_term = lax.dot_general(
        down_grad, cross_down, (((1,), (1,)), ((), ())), preferred_element_type=jnp.float32
    )
    input_grad = (cotangent * (gate_scale + 1.0) + back_term).astype(jnp.bfloat16)
    bottom_grad = input_grad[:, :row_width]
    row_grads = input_grad[:, row_width:].reshape(lookup_count, row_width)
    outgoing = jnp.zeros((slot_count, row_width), jnp.bfloat16).at[buffer_place].set(row_grads)
    incoming = lax.all_to_all(
        outgoing.reshape(owner_count, capacity, row_width),
        "emb",
        split_axis=0,
        concat_axis=0,
        tiled=True,
    )
    local_grad = add_rows(
        table_count * rows_local,
        received_flat,
        incoming.reshape(slot_count, row_width),
        jnp.float32,
    )
    summed_grad = lax.psum(local_grad.astype(jnp.bfloat16), "grp").astype(jnp.float32)
    table_grad = summed_grad.reshape(table_count, rows_local, row_width)
    bias_local = jnp.sum(scaled, axis=0)
    bias_grad = lax.psum(bias_local, ("grp", "emb"))
    return (table_grad, bottom_grad, bias_grad)


def solution(mesh):
    placed = (
        P(("grp", "emb"), None),
        P(("grp", "emb"), None),
        P(("grp", "emb"), None),
        P(("grp", "emb")),
        P(("grp", "emb")),
        P(None, "emb", None),
        P(),
        P(),
        P(),
        P(),
        P(),
    )
    return jax.shard_map(
        local,
        mesh=mesh,
        in_specs=placed,
        out_specs=(P(None, "emb", None), P(("grp", "emb"), None), P()),
        check_vma=False,
    )
```

```python
import functools

import jax
import jax.numpy as jnp
from jax import lax
from jax.experimental import pallas as pl
from jax.experimental.pallas import tpu as pltpu
from jax.sharding import PartitionSpec as P

def _row_block(rows):
    if rows <= 4096:
        return rows
    for size in range(4096, 7, -8):
        if rows % size == 0:
            return size
    return rows


def _chunk_of(count):
    for size in (512, 384, 256, 128):
        if count % size == 0:
            return size
    return 512


def _select_kernel(chunk, chunks, right_ref, data_ref, out_ref):
    block = out_ref.shape[0]
    left = lax.broadcasted_iota(jnp.int32, (block, 1), 0) + pl.program_id(0) * block

    def step(j, acc):
        start = pl.multiple_of(j * chunk, chunk)
        right = right_ref[:, pl.ds(start, chunk)]
        picks = jnp.where(left == right, 1.0, 0.0).astype(data_ref.dtype)
        part = data_ref[pl.ds(start, chunk), :]
        return acc + jnp.dot(picks, part, preferred_element_type=jnp.float32)

    acc = jnp.zeros(out_ref.shape, jnp.float32)
    acc = lax.fori_loop(0, chunks, step, acc)
    out_ref[...] = acc.astype(out_ref.dtype)


def add_rows(rows, right, data, out_dtype):
    count, width = data.shape
    chunk = _chunk_of(count)
    padded = -(-count // chunk) * chunk
    if padded != count:
        right = jnp.pad(right, (0, padded - count), constant_values=-1)
        data = jnp.pad(data, ((0, padded - count), (0, 0)))
    right = right.reshape(1, padded)
    block = _row_block(rows)
    return pl.pallas_call(
        functools.partial(_select_kernel, chunk, padded // chunk),
        out_shape=jax.ShapeDtypeStruct((rows, width), out_dtype),
        grid=(rows // block,),
        in_specs=[
            pl.BlockSpec((1, padded), lambda i: (0, 0)),
            pl.BlockSpec((padded, width), lambda i: (0, 0)),
        ],
        out_specs=pl.BlockSpec((block, width), lambda i: (i, 0)),
        cost_estimate=pl.CostEstimate(
            flops=2 * rows * padded * width,
            transcendentals=0,
            bytes_accessed=padded * width * data.dtype.itemsize
            + rows * width * jnp.dtype(out_dtype).itemsize,
        ),
    )(right, data)


def local(
    bottom_out,
    owner_ids,
    row_ids,
    positions,
    labels,
    tables,
    cross_down,
    cross_up,
    cross_bias,
    out_weight,
    position_bias,
):
    sample_count, table_count = row_ids.shape
    rows_local = tables.shape[1]
    row_width = tables.shape[2]
    owner_count = lax.axis_size("emb")
    capacity = 3 * sample_count * table_count // (2 * owner_count)
    lookup_count = sample_count * table_count
    owners = owner_ids.reshape(sample_count, table_count)
    flat_owner = owners.reshape(-1)
    local_grid = jnp.arange(table_count, dtype=jnp.int32)[None, :] * rows_local + row_ids
    local_index = local_grid.reshape(-1)
    owner_marks = (flat_owner[:, None] == jnp.arange(owner_count, dtype=jnp.int32)[None, :]).astype(
        jnp.int32
    )
    ranking = jnp.cumsum(owner_marks, axis=0) - 1
    slot_index = jnp.sum(ranking * owner_marks, axis=1)
    buffer_place = flat_owner * capacity + slot_index
    flat_table = tables.reshape(table_count * rows_local, row_width)
    request = jnp.zeros((owner_count * capacity,), jnp.int32).at[buffer_place].set(local_index)
    request = request.reshape(owner_count, capacity)
    received = lax.all_to_all(request, "emb", split_axis=0, concat_axis=0, tiled=True)
    slot_count = owner_count * capacity
    received_flat = received.reshape(-1)
    fetched = flat_table[received]
    arrived = lax.all_to_all(fetched, "emb", split_axis=0, concat_axis=0, tiled=True)
    pooled = arrived.reshape(slot_count, row_width)[buffer_place].reshape(
        sample_count, table_count * row_width
    )
    first = jnp.concatenate([bottom_out, pooled], axis=1)
    first_wide = first.astype(jnp.float32)
    weight_row = out_weight.astype(jnp.float32)
    reduced = jnp.dot(first, cross_down, preferred_element_type=jnp.float32).astype(jnp.bfloat16)
    gate_scale = jnp.dot(reduced, cross_up, preferred_element_type=jnp.float32) + cross_bias
    crossed = first_wide * gate_scale + first_wide
    position_marks = (
        positions[:, None] == jnp.arange(position_bias.shape[0], dtype=jnp.int32)[None, :]
    ).astype(jnp.float32)
    logit = jnp.sum(crossed * weight_row[None, :], axis=1) + jnp.sum(
        position_marks * position_bias[None, :], axis=1
    )
    err = jax.nn.sigmoid(logit) - labels.astype(jnp.float32)
    cotangent = err[:, None] * weight_row[None, :]
    scaled = cotangent * first_wide
    down_grad = lax.dot_general(
        scaled.astype(jnp.bfloat16),
        cross_up,
        (((1,), (1,)), ((), ())),
        preferred_element_type=jnp.float32,
    ).astype(jnp.bfloat16)
    back_term = lax.dot_general(
        down_grad, cross_down, (((1,), (1,)), ((), ())), preferred_element_type=jnp.float32
    )
    input_grad = (cotangent * (gate_scale + 1.0) + back_term).astype(jnp.bfloat16)
    bottom_grad = input_grad[:, :row_width]
    row_grads = input_grad[:, row_width:].reshape(lookup_count, row_width)
    outgoing = jnp.zeros((slot_count, row_width), jnp.bfloat16).at[buffer_place].set(row_grads)
    incoming = lax.all_to_all(
        outgoing.reshape(owner_count, capacity, row_width),
        "emb",
        split_axis=0,
        concat_axis=0,
        tiled=True,
    )
    local_grad = add_rows(
        table_count * rows_local,
        received_flat,
        incoming.reshape(slot_count, row_width),
        jnp.bfloat16,
    )
    summed_grad = lax.psum(local_grad, "grp").astype(jnp.float32)
    table_grad = summed_grad.reshape(table_count, rows_local, row_width)
    bias_local = jnp.sum(scaled, axis=0)
    bias_grad = lax.psum(bias_local, ("grp", "emb"))
    return (table_grad, bottom_grad, bias_grad)


def solution(mesh):
    placed = (
        P(("grp", "emb"), None),
        P(("grp", "emb"), None),
        P(("grp", "emb"), None),
        P(("grp", "emb")),
        P(("grp", "emb")),
        P(None, "emb", None),
        P(),
        P(),
        P(),
        P(),
        P(),
    )
    return jax.shard_map(
        local,
        mesh=mesh,
        in_specs=placed,
        out_specs=(P(None, "emb", None), P(("grp", "emb"), None), P()),
        check_vma=False,
    )
```

```python
import functools

import jax
import jax.numpy as jnp
from jax import lax
from jax.experimental import pallas as pl
from jax.experimental.pallas import tpu as pltpu
from jax.sharding import PartitionSpec as P

def _row_block(rows):
    if rows <= 4096:
        return rows
    for size in range(4096, 7, -8):
        if rows % size == 0:
            return size
    return rows


def _chunk_of(count):
    for size in (512, 384, 256, 128):
        if count % size == 0:
            return size
    return 512


def _select_kernel(chunk, chunks, right_ref, data_ref, out_ref):
    block = out_ref.shape[0]
    left = lax.broadcasted_iota(jnp.int32, (block, 1), 0) + pl.program_id(0) * block

    def step(j, acc):
        start = pl.multiple_of(j * chunk, chunk)
        right = right_ref[:, pl.ds(start, chunk)]
        picks = jnp.where(left == right, 1.0, 0.0).astype(data_ref.dtype)
        part = data_ref[pl.ds(start, chunk), :]
        return acc + jnp.dot(picks, part, preferred_element_type=jnp.float32)

    acc = jnp.zeros(out_ref.shape, jnp.float32)
    acc = lax.fori_loop(0, chunks, step, acc)
    out_ref[...] = acc.astype(out_ref.dtype)


def add_rows(rows, right, data, out_dtype):
    count, width = data.shape
    chunk = _chunk_of(count)
    padded = -(-count // chunk) * chunk
    if padded != count:
        right = jnp.pad(right, (0, padded - count), constant_values=-1)
        data = jnp.pad(data, ((0, padded - count), (0, 0)))
    right = right.reshape(1, padded)
    block = _row_block(rows)
    return pl.pallas_call(
        functools.partial(_select_kernel, chunk, padded // chunk),
        out_shape=jax.ShapeDtypeStruct((rows, width), out_dtype),
        grid=(rows // block,),
        in_specs=[
            pl.BlockSpec((1, padded), lambda i: (0, 0)),
            pl.BlockSpec((padded, width), lambda i: (0, 0)),
        ],
        out_specs=pl.BlockSpec((block, width), lambda i: (i, 0)),
        cost_estimate=pl.CostEstimate(
            flops=2 * rows * padded * width,
            transcendentals=0,
            bytes_accessed=padded * width * data.dtype.itemsize
            + rows * width * jnp.dtype(out_dtype).itemsize,
        ),
    )(right, data)


def local(
    bottom_out,
    owner_ids,
    row_ids,
    positions,
    labels,
    tables,
    cross_down,
    cross_up,
    cross_bias,
    out_weight,
    position_bias,
):
    sample_count, table_count = row_ids.shape
    rows_local = tables.shape[1]
    row_width = tables.shape[2]
    owner_count = lax.axis_size("emb")
    capacity = 3 * sample_count * table_count // (2 * owner_count)
    lookup_count = sample_count * table_count
    owners = owner_ids.reshape(sample_count, table_count)
    flat_owner = owners.reshape(-1)
    local_grid = jnp.arange(table_count, dtype=jnp.int32)[None, :] * rows_local + row_ids
    local_index = local_grid.reshape(-1)
    owner_marks = (flat_owner[:, None] == jnp.arange(owner_count, dtype=jnp.int32)[None, :]).astype(
        jnp.int32
    )
    ranking = jnp.cumsum(owner_marks, axis=0) - 1
    slot_index = jnp.sum(ranking * owner_marks, axis=1)
    buffer_place = flat_owner * capacity + slot_index
    flat_table = tables.reshape(table_count * rows_local, row_width)
    request = jnp.zeros((owner_count * capacity,), jnp.int32).at[buffer_place].set(local_index)
    request = request.reshape(owner_count, capacity)
    received = lax.all_to_all(request, "emb", split_axis=0, concat_axis=0, tiled=True)
    slot_count = owner_count * capacity
    received_flat = received.reshape(-1)
    fetched = flat_table[received]
    arrived = lax.all_to_all(fetched, "emb", split_axis=0, concat_axis=0, tiled=True)
    pooled = arrived.reshape(slot_count, row_width)[buffer_place].reshape(
        sample_count, table_count * row_width
    )
    first = jnp.concatenate([bottom_out, pooled], axis=1)
    first_wide = first.astype(jnp.float32)
    weight_row = out_weight.astype(jnp.float32)
    reduced = jnp.dot(first, cross_down, preferred_element_type=jnp.float32).astype(jnp.bfloat16)
    gate_scale = jnp.dot(reduced, cross_up, preferred_element_type=jnp.float32) + cross_bias
    crossed = first_wide * gate_scale + first_wide
    position_marks = (
        positions[:, None] == jnp.arange(position_bias.shape[0], dtype=jnp.int32)[None, :]
    ).astype(jnp.float32)
    logit = jnp.sum(crossed * weight_row[None, :], axis=1) + jnp.sum(
        position_marks * position_bias[None, :], axis=1
    )
    err = jax.nn.sigmoid(logit) - labels.astype(jnp.float32)
    cotangent = err[:, None] * weight_row[None, :]
    scaled = cotangent * first_wide
    down_grad = lax.dot_general(
        scaled.astype(jnp.bfloat16),
        cross_up,
        (((1,), (1,)), ((), ())),
        preferred_element_type=jnp.float32,
    ).astype(jnp.bfloat16)
    back_term = lax.dot_general(
        down_grad, cross_down, (((1,), (1,)), ((), ())), preferred_element_type=jnp.float32
    )
    input_grad = (cotangent * (gate_scale + 1.0) + back_term).astype(jnp.bfloat16)
    bottom_grad = input_grad[:, :row_width]
    row_grads = input_grad[:, row_width:].reshape(lookup_count, row_width)
    outgoing = jnp.zeros((slot_count, row_width), jnp.bfloat16).at[buffer_place].set(row_grads)
    incoming = lax.all_to_all(
        outgoing.reshape(owner_count, capacity, row_width),
        "emb",
        split_axis=0,
        concat_axis=0,
        tiled=True,
    )
    bias_local = jnp.sum(scaled, axis=0)
    bias_local, bottom_grad, incoming = lax.optimization_barrier((bias_local, bottom_grad, incoming))
    local_grad = add_rows(
        table_count * rows_local,
        received_flat,
        incoming.reshape(slot_count, row_width),
        jnp.bfloat16,
    )
    summed_grad = lax.psum(local_grad, "grp").astype(jnp.float32)
    table_grad = summed_grad.reshape(table_count, rows_local, row_width)
    bias_grad = lax.psum(bias_local, ("grp", "emb"))
    return (table_grad, bottom_grad, bias_grad)


def solution(mesh):
    placed = (
        P(("grp", "emb"), None),
        P(("grp", "emb"), None),
        P(("grp", "emb"), None),
        P(("grp", "emb")),
        P(("grp", "emb")),
        P(None, "emb", None),
        P(),
        P(),
        P(),
        P(),
        P(),
    )
    return jax.shard_map(
        local,
        mesh=mesh,
        in_specs=placed,
        out_specs=(P(None, "emb", None), P(("grp", "emb"), None), P()),
        check_vma=False,
    )
```

```python
import functools

import jax
import jax.numpy as jnp
from jax import lax
from jax.experimental import pallas as pl
from jax.experimental.pallas import tpu as pltpu
from jax.sharding import PartitionSpec as P

def _row_block(rows):
    if rows <= 4096:
        return rows
    for size in range(4096, 7, -8):
        if rows % size == 0:
            return size
    return rows


def _chunk_of(count):
    for size in (1664, 512, 384, 256, 128):
        if count % size == 0:
            return size
    return 512


def _select_kernel(chunk, chunks, right_ref, data_ref, out_ref):
    block = out_ref.shape[0]
    left = lax.broadcasted_iota(jnp.int32, (block, 1), 0) + pl.program_id(0) * block

    def step(j, acc):
        start = pl.multiple_of(j * chunk, chunk)
        right = right_ref[:, pl.ds(start, chunk)]
        picks = jnp.where(left == right, 1.0, 0.0).astype(data_ref.dtype)
        part = data_ref[pl.ds(start, chunk), :]
        return acc + jnp.dot(picks, part, preferred_element_type=jnp.float32)

    acc = jnp.zeros(out_ref.shape, jnp.float32)
    acc = lax.fori_loop(0, chunks, step, acc)
    out_ref[...] = acc.astype(out_ref.dtype)


def add_rows(rows, right, data, out_dtype):
    count, width = data.shape
    chunk = _chunk_of(count)
    padded = -(-count // chunk) * chunk
    if padded != count:
        right = jnp.pad(right, (0, padded - count), constant_values=-1)
        data = jnp.pad(data, ((0, padded - count), (0, 0)))
    right = right.reshape(1, padded)
    block = _row_block(rows)
    return pl.pallas_call(
        functools.partial(_select_kernel, chunk, padded // chunk),
        out_shape=jax.ShapeDtypeStruct((rows, width), out_dtype),
        grid=(rows // block,),
        in_specs=[
            pl.BlockSpec((1, padded), lambda i: (0, 0)),
            pl.BlockSpec((padded, width), lambda i: (0, 0)),
        ],
        out_specs=pl.BlockSpec((block, width), lambda i: (i, 0)),
        cost_estimate=pl.CostEstimate(
            flops=2 * rows * padded * width,
            transcendentals=0,
            bytes_accessed=padded * width * data.dtype.itemsize
            + rows * width * jnp.dtype(out_dtype).itemsize,
        ),
    )(right, data)


def local(
    bottom_out,
    owner_ids,
    row_ids,
    positions,
    labels,
    tables,
    cross_down,
    cross_up,
    cross_bias,
    out_weight,
    position_bias,
):
    sample_count, table_count = row_ids.shape
    rows_local = tables.shape[1]
    row_width = tables.shape[2]
    owner_count = lax.axis_size("emb")
    capacity = 3 * sample_count * table_count // (2 * owner_count)
    lookup_count = sample_count * table_count
    owners = owner_ids.reshape(sample_count, table_count)
    flat_owner = owners.reshape(-1)
    local_grid = jnp.arange(table_count, dtype=jnp.int32)[None, :] * rows_local + row_ids
    local_index = local_grid.reshape(-1)
    owner_marks = (flat_owner[:, None] == jnp.arange(owner_count, dtype=jnp.int32)[None, :]).astype(
        jnp.int32
    )
    ranking = jnp.cumsum(owner_marks, axis=0) - 1
    slot_index = jnp.sum(ranking * owner_marks, axis=1)
    buffer_place = flat_owner * capacity + slot_index
    flat_table = tables.reshape(table_count * rows_local, row_width)
    request = jnp.zeros((owner_count * capacity,), jnp.int32).at[buffer_place].set(local_index)
    request = request.reshape(owner_count, capacity)
    received = lax.all_to_all(request, "emb", split_axis=0, concat_axis=0, tiled=True)
    slot_count = owner_count * capacity
    received_flat = received.reshape(-1)
    fetched = flat_table[received]
    arrived = lax.all_to_all(fetched, "emb", split_axis=0, concat_axis=0, tiled=True)
    pooled = arrived.reshape(slot_count, row_width)[buffer_place].reshape(
        sample_count, table_count * row_width
    )
    first = jnp.concatenate([bottom_out, pooled], axis=1)
    first_wide = first.astype(jnp.float32)
    weight_row = out_weight.astype(jnp.float32)
    reduced = jnp.dot(first, cross_down, preferred_element_type=jnp.float32).astype(jnp.bfloat16)
    gate_scale = jnp.dot(reduced, cross_up, preferred_element_type=jnp.float32) + cross_bias
    crossed = first_wide * gate_scale + first_wide
    position_marks = (
        positions[:, None] == jnp.arange(position_bias.shape[0], dtype=jnp.int32)[None, :]
    ).astype(jnp.float32)
    logit = jnp.sum(crossed * weight_row[None, :], axis=1) + jnp.sum(
        position_marks * position_bias[None, :], axis=1
    )
    err = jax.nn.sigmoid(logit) - labels.astype(jnp.float32)
    cotangent = err[:, None] * weight_row[None, :]
    scaled = cotangent * first_wide
    down_grad = lax.dot_general(
        scaled.astype(jnp.bfloat16),
        cross_up,
        (((1,), (1,)), ((), ())),
        preferred_element_type=jnp.float32,
    ).astype(jnp.bfloat16)
    back_term = lax.dot_general(
        down_grad, cross_down, (((1,), (1,)), ((), ())), preferred_element_type=jnp.float32
    )
    input_grad = (cotangent * (gate_scale + 1.0) + back_term).astype(jnp.bfloat16)
    bottom_grad = input_grad[:, :row_width]
    row_grads = input_grad[:, row_width:].reshape(lookup_count, row_width)
    outgoing = jnp.zeros((slot_count, row_width), jnp.bfloat16).at[buffer_place].set(row_grads)
    incoming = lax.all_to_all(
        outgoing.reshape(owner_count, capacity, row_width),
        "emb",
        split_axis=0,
        concat_axis=0,
        tiled=True,
    )
    bias_local = jnp.sum(scaled, axis=0)
    bias_local, bottom_grad, incoming = lax.optimization_barrier((bias_local, bottom_grad, incoming))
    local_grad = add_rows(
        table_count * rows_local,
        received_flat,
        incoming.reshape(slot_count, row_width),
        jnp.bfloat16,
    )
    summed_grad = lax.psum(local_grad, "grp").astype(jnp.float32)
    table_grad = summed_grad.reshape(table_count, rows_local, row_width)
    bias_grad = lax.psum(bias_local, ("grp", "emb"))
    return (table_grad, bottom_grad, bias_grad)


def solution(mesh):
    placed = (
        P(("grp", "emb"), None),
        P(("grp", "emb"), None),
        P(("grp", "emb"), None),
        P(("grp", "emb")),
        P(("grp", "emb")),
        P(None, "emb", None),
        P(),
        P(),
        P(),
        P(),
        P(),
    )
    return jax.shard_map(
        local,
        mesh=mesh,
        in_specs=placed,
        out_specs=(P(None, "emb", None), P(("grp", "emb"), None), P()),
        check_vma=False,
    )
```

```python
import functools

import jax
import jax.numpy as jnp
from jax import lax
from jax.experimental import pallas as pl
from jax.experimental.pallas import tpu as pltpu
from jax.sharding import PartitionSpec as P

def _row_block(rows):
    if rows <= 4096:
        return rows
    for size in range(4096, 7, -8):
        if rows % size == 0:
            return size
    return rows


def _chunk_of(count):
    for size in (4992, 1664, 512, 384, 256, 128):
        if count % size == 0:
            return size
    return 512


def _select_kernel(chunk, chunks, right_ref, data_ref, out_ref):
    block = out_ref.shape[0]
    left = lax.broadcasted_iota(jnp.int32, (block, 1), 0) + pl.program_id(0) * block

    def step(j, acc):
        start = pl.multiple_of(j * chunk, chunk)
        right = right_ref[:, pl.ds(start, chunk)]
        picks = jnp.where(left == right, 1.0, 0.0).astype(data_ref.dtype)
        part = data_ref[pl.ds(start, chunk), :]
        return acc + jnp.dot(picks, part, preferred_element_type=jnp.float32)

    acc = jnp.zeros(out_ref.shape, jnp.float32)
    acc = lax.fori_loop(0, chunks, step, acc)
    out_ref[...] = acc.astype(out_ref.dtype)


def add_rows(rows, right, data, out_dtype):
    count, width = data.shape
    chunk = _chunk_of(count)
    padded = -(-count // chunk) * chunk
    if padded != count:
        right = jnp.pad(right, (0, padded - count), constant_values=-1)
        data = jnp.pad(data, ((0, padded - count), (0, 0)))
    right = right.reshape(1, padded)
    block = _row_block(rows)
    return pl.pallas_call(
        functools.partial(_select_kernel, chunk, padded // chunk),
        out_shape=jax.ShapeDtypeStruct((rows, width), out_dtype),
        grid=(rows // block,),
        in_specs=[
            pl.BlockSpec((1, padded), lambda i: (0, 0)),
            pl.BlockSpec((padded, width), lambda i: (0, 0)),
        ],
        out_specs=pl.BlockSpec((block, width), lambda i: (i, 0)),
        cost_estimate=pl.CostEstimate(
            flops=2 * rows * padded * width,
            transcendentals=0,
            bytes_accessed=padded * width * data.dtype.itemsize
            + rows * width * jnp.dtype(out_dtype).itemsize,
        ),
    )(right, data)


def local(
    bottom_out,
    owner_ids,
    row_ids,
    positions,
    labels,
    tables,
    cross_down,
    cross_up,
    cross_bias,
    out_weight,
    position_bias,
):
    sample_count, table_count = row_ids.shape
    rows_local = tables.shape[1]
    row_width = tables.shape[2]
    owner_count = lax.axis_size("emb")
    capacity = 3 * sample_count * table_count // (2 * owner_count)
    lookup_count = sample_count * table_count
    owners = owner_ids.reshape(sample_count, table_count)
    flat_owner = owners.reshape(-1)
    local_grid = jnp.arange(table_count, dtype=jnp.int32)[None, :] * rows_local + row_ids
    local_index = local_grid.reshape(-1)
    owner_marks = (flat_owner[:, None] == jnp.arange(owner_count, dtype=jnp.int32)[None, :]).astype(
        jnp.int32
    )
    ranking = jnp.cumsum(owner_marks, axis=0) - 1
    slot_index = jnp.sum(ranking * owner_marks, axis=1)
    buffer_place = flat_owner * capacity + slot_index
    flat_table = tables.reshape(table_count * rows_local, row_width)
    request = jnp.zeros((owner_count * capacity,), jnp.int32).at[buffer_place].set(local_index)
    request = request.reshape(owner_count, capacity)
    received = lax.all_to_all(request, "emb", split_axis=0, concat_axis=0, tiled=True)
    slot_count = owner_count * capacity
    received_flat = received.reshape(-1)
    fetched = flat_table[received]
    arrived = lax.all_to_all(fetched, "emb", split_axis=0, concat_axis=0, tiled=True)
    pooled = arrived.reshape(slot_count, row_width)[buffer_place].reshape(
        sample_count, table_count * row_width
    )
    first = jnp.concatenate([bottom_out, pooled], axis=1)
    first_wide = first.astype(jnp.float32)
    weight_row = out_weight.astype(jnp.float32)
    reduced = jnp.dot(first, cross_down, preferred_element_type=jnp.float32).astype(jnp.bfloat16)
    gate_scale = jnp.dot(reduced, cross_up, preferred_element_type=jnp.float32) + cross_bias
    crossed = first_wide * gate_scale + first_wide
    position_marks = (
        positions[:, None] == jnp.arange(position_bias.shape[0], dtype=jnp.int32)[None, :]
    ).astype(jnp.float32)
    logit = jnp.sum(crossed * weight_row[None, :], axis=1) + jnp.sum(
        position_marks * position_bias[None, :], axis=1
    )
    err = jax.nn.sigmoid(logit) - labels.astype(jnp.float32)
    cotangent = err[:, None] * weight_row[None, :]
    scaled = cotangent * first_wide
    down_grad = lax.dot_general(
        scaled.astype(jnp.bfloat16),
        cross_up,
        (((1,), (1,)), ((), ())),
        preferred_element_type=jnp.float32,
    ).astype(jnp.bfloat16)
    back_term = lax.dot_general(
        down_grad, cross_down, (((1,), (1,)), ((), ())), preferred_element_type=jnp.float32
    )
    input_grad = (cotangent * (gate_scale + 1.0) + back_term).astype(jnp.bfloat16)
    bottom_grad = input_grad[:, :row_width]
    row_grads = input_grad[:, row_width:].reshape(lookup_count, row_width)
    outgoing = jnp.zeros((slot_count, row_width), jnp.bfloat16).at[buffer_place].set(row_grads)
    incoming = lax.all_to_all(
        outgoing.reshape(owner_count, capacity, row_width),
        "emb",
        split_axis=0,
        concat_axis=0,
        tiled=True,
    )
    bias_local = jnp.sum(scaled, axis=0)
    bias_local, bottom_grad, incoming = lax.optimization_barrier((bias_local, bottom_grad, incoming))
    local_grad = add_rows(
        table_count * rows_local,
        received_flat,
        incoming.reshape(slot_count, row_width),
        jnp.bfloat16,
    )
    summed_grad = lax.psum(local_grad, "grp").astype(jnp.float32)
    table_grad = summed_grad.reshape(table_count, rows_local, row_width)
    bias_grad = lax.psum(bias_local, ("grp", "emb"))
    return (table_grad, bottom_grad, bias_grad)


def solution(mesh):
    placed = (
        P(("grp", "emb"), None),
        P(("grp", "emb"), None),
        P(("grp", "emb"), None),
        P(("grp", "emb")),
        P(("grp", "emb")),
        P(None, "emb", None),
        P(),
        P(),
        P(),
        P(),
        P(),
    )
    return jax.shard_map(
        local,
        mesh=mesh,
        in_specs=placed,
        out_specs=(P(None, "emb", None), P(("grp", "emb"), None), P()),
        check_vma=False,
    )
```
